128 devices in a mesh: fsdp: 16 (over x_hi, y, core), dp: 8 (over z, x_lo).
Axes of the slice: x: 4 (x_hi: 2, x_lo: 2; x = x_hi * 2 + x_lo), y: 4, z: 4, core: 2. Of those that a mesh axis runs over, the one named last changes fastest.
Arguments:
- hidden: bfloat16 [12288, 8192], P('fsdp', 'dp'), may hold values from -6 to 6
- combine_weight: float32 [12288], P('fsdp'), may hold values from 0.2 to 1
- down_weight: bfloat16 [4096, 2, 8192], P('fsdp', None, 'dp'), may hold values from -0.0625 to 0.0625
- cotangent: bfloat16 [12288, 4096], P('fsdp', 'dp'), may hold values from -6 to 6
- expert_rows: int32 [16, 2], P('fsdp'), may hold values from 1 to 640, as said below
- block_expert: int32 [96], P('fsdp'), may hold values from 0 to 1, as said below
- slot_token: int32 [12288], P('fsdp'), may hold values from 0 to 767, as said below
Outputs:
- expert_out: bfloat16 [12288, 4096], P('fsdp', 'dp')
- grad_hidden: bfloat16 [12288, 8192], P('fsdp', 'dp')
- grad_down: bfloat16 [4096, 2, 8192], P('fsdp', None, 'dp')
The draws below stay inside these ranges and needn't reach their ends.
Inputs may be any that keep to these rules, and one draw needn't show every extreme that they name: `expert_rows`: row i gives the live rows of the first and the second expert in group i; the first expert's rows fill blocks from block 0 on, the second's start at the next free block, each takes ceil(rows / 128) blocks and both together at most 6; in every draw some group uses all 6 blocks. `block_expert`: within each group: 0 for the first expert's blocks, 1 for every later block; blocks past both experts' have no live rows. `slot_token`: tokens counted within the slot's group; the live slots of one expert in a group name different tokens of that group; slots that are not live hold arbitrary tokens.
All inputs are finite; a program needn't handle non-finite values.
Results may differ from the reference program's by a relative error of at most 0.014.
Values may be sent and summed in bfloat16 or wider, within the bound.
No kernel may reach another device: no remote copies, remote signals or barrier semaphores. Data moves between devices by JAX's collectives and lax.ppermute only.
A program may use at most 192 MiB of HBM per device.

```python
import math
import jax
import jax.numpy as jnp
from jax import lax

D = 4096
FF = 8192
EXPERTS = 2
BLK = 128
NB_DEV = 6
SLOTS = 12288
TOKENS = 12288
BLOCKS = 96
N_FSDP = 16
N_DP = 8


def layout(key):
    group_total = BLOCKS // NB_DEV
    slot_total = NB_DEV * BLK
    fuller = jax.random.randint(jax.random.fold_in(key, 11), (), 0, group_total)

    def single(group_index):
        subkey = jax.random.fold_in(jax.random.fold_in(key, 17), group_index)
        keys = jax.random.split(subkey, 6)
        is_full = group_index == fuller
        first_blocks = jax.random.randint(keys[0], (), 1, NB_DEV)
        second_blocks = jax.random.randint(keys[1], (), 1, NB_DEV - first_blocks + 1)
        first_blocks = jnp.where(is_full, NB_DEV - 1, first_blocks)
        second_blocks = jnp.where(is_full, 1, second_blocks)
        first_rows = (first_blocks - 1) * BLK + jax.random.randint(keys[2], (), 1, BLK + 1)
        first_rows = jnp.where(is_full, first_blocks * BLK, first_rows)
        second_rows = (second_blocks - 1) * BLK + jax.random.randint(keys[3], (), 1, BLK + 1)
        order_first = jax.random.permutation(keys[4], slot_total)
        order_second = jax.random.permutation(keys[5], slot_total)
        positions = jnp.arange(slot_total, dtype=jnp.int32)
        later = jnp.clip(positions - first_blocks * BLK, 0, slot_total - 1)
        tokens = jnp.where(positions < first_blocks * BLK, order_first[positions], order_second[later])
        tokens = jnp.where(is_full, order_first[positions], tokens)
        experts = jnp.where(jnp.arange(NB_DEV, dtype=jnp.int32) < first_blocks, 0, 1)
        rows_pair = jnp.stack([first_rows, second_rows])
        return (rows_pair.astype(jnp.int32), experts.astype(jnp.int32), tokens.astype(jnp.int32))
    return jax.vmap(single)(jnp.arange(group_total, dtype=jnp.int32))


def draw_expert_rows(key, part):
    return layout(key)[0]


def draw_block_expert(key, part):
    return layout(key)[1].reshape(-1)


def draw_slot_token(key, part):
    return layout(key)[2].reshape(-1)


def steps_of(own_key, shape, cuts, low, high):
    loudness, own = 1.0, jax.random.fold_in(own_key, 6)
    for dim, blocks in cuts:
        draws = jnp.exp(jax.random.uniform(jax.random.fold_in(own, dim), (blocks,), jnp.float32, low / len(cuts), high / len(cuts)))
        loudness = loudness * jnp.repeat(draws, shape[dim] // blocks).reshape([-1 if axis == dim else 1 for axis in range(len(shape))])
    return loudness


def noise(rng, dims, spread, most, pieces=(), kind=jnp.bfloat16):
    factor_of = steps_of(rng, dims, pieces, -0.22, 0.18) if pieces else 1.0
    result = jax.random.normal(rng, dims, jnp.float32) * spread * factor_of
    return jnp.minimum(jnp.maximum(result, -most), most).astype(kind)


def setup_inputs(seed: int = 0) -> dict:
    arg_keys = jax.random.split(jax.random.key(seed), 8)
    return {
        "hidden": noise(arg_keys[0], (SLOTS, FF), 1.0, 6.0, ((0, 16), (1, 8))),
        "combine_weight": jnp.clip(0.2 + 0.8 * jax.random.uniform(arg_keys[1], (SLOTS,), jnp.float32) ** steps_of(arg_keys[1], (SLOTS,), ((0, 16),), -0.2, 0.2), 0.2, 1.0),
        "down_weight": noise(arg_keys[2], (D, EXPERTS, FF), FF ** -0.5, 0.0625, ((0, 16), (2, 8))),
        "cotangent": noise(arg_keys[3], (TOKENS, D), 1.0, 6.0, ((0, 16), (1, 8))),
        "expert_rows": draw_expert_rows(jax.random.fold_in(arg_keys[7], 71), 0),
        "block_expert": draw_block_expert(jax.random.fold_in(arg_keys[7], 71), 0),
        "slot_token": draw_slot_token(jax.random.fold_in(arg_keys[7], 71), 0),
    }


def reference(hidden, combine_weight, down_weight, cotangent, expert_rows, block_expert, slot_token):
    group_count = N_FSDP
    hidden_groups = N_DP
    slot_count = NB_DEV * BLK
    group_width = FF // hidden_groups
    positions = jnp.arange(slot_count, dtype=jnp.int32)
    blocks = positions // BLK
    expert_ids = jnp.arange(EXPERTS, dtype=jnp.int32)

    def per_group(running, group_index):
        live_rows = lax.dynamic_index_in_dim(expert_rows, group_index, 0, keepdims=False)
        first_blocks = (live_rows[0] + BLK - 1) // BLK
        second_blocks = (live_rows[1] + BLK - 1) // BLK
        live = jnp.where(blocks < first_blocks, positions < live_rows[0], (blocks < first_blocks + second_blocks) & (positions - first_blocks * BLK < live_rows[1]))
        offset = (group_index * slot_count).astype(jnp.int32)
        hid_rows = lax.dynamic_slice_in_dim(hidden, offset, slot_count, 0)
        slot_scale = lax.dynamic_slice_in_dim(combine_weight, offset, slot_count, 0) * live.astype(jnp.float32)
        tokens = lax.dynamic_slice_in_dim(slot_token, offset, slot_count, 0)
        experts = lax.dynamic_slice_in_dim(block_expert, (group_index * NB_DEV).astype(jnp.int32), NB_DEV, 0)
        cot_rows = lax.dynamic_slice_in_dim(cotangent, offset, slot_count, 0)
        slot_cot = (slot_scale[:, None] * cot_rows[tokens].astype(jnp.float32)).astype(jnp.bfloat16)
        panels = jnp.take(down_weight, experts, axis=1)
        hid_split = hid_rows.reshape(NB_DEV, BLK, hidden_groups, group_width).astype(jnp.float32)
        panel_split = panels.reshape(D, NB_DEV, hidden_groups, group_width).astype(jnp.float32)
        slot_out = jnp.einsum('btjh,dbjh->jbtd', hid_split, panel_split).reshape(hidden_groups, slot_count, D)

        def combine(part_out):
            return jnp.zeros((slot_count, D), jnp.float32).at[tokens].add(slot_scale[:, None] * part_out)
        token_part = jax.vmap(combine)(slot_out).astype(jnp.bfloat16)
        token_part = lax.optimization_barrier(token_part)
        expert_out = lax.optimization_barrier(jnp.sum(token_part.astype(jnp.float32), axis=0)).astype(jnp.bfloat16)
        cot_blocks = slot_cot.reshape(NB_DEV, BLK, D).astype(jnp.float32)
        grad_hidden = jnp.einsum('btd,dbf->btf', cot_blocks, panels.astype(jnp.float32)).reshape(slot_count, FF)
        products = jnp.einsum('btd,btf->bdf', cot_blocks, hid_rows.reshape(NB_DEV, BLK, FF).astype(jnp.float32))
        onehot = (experts[:, None] == expert_ids[None, :]).astype(jnp.float32)
        device_grad = jnp.einsum('be,bdf->def', onehot, products, precision=lax.Precision.HIGHEST)
        device_grad = lax.optimization_barrier(device_grad.astype(jnp.bfloat16))
        running = running + device_grad.astype(jnp.float32)
        return (running, (expert_out, grad_hidden.astype(jnp.bfloat16)))
    start_grad = jnp.zeros((D, EXPERTS, FF), jnp.float32)
    summed, (outputs, hidden_grads) = lax.scan(per_group, start_grad, jnp.arange(group_count, dtype=jnp.int32))
    grad_down = (summed * (1.0 / math.sqrt(SLOTS))).astype(jnp.bfloat16)
    return (outputs.reshape(TOKENS, D), hidden_grads.reshape(SLOTS, FF), grad_down)
```

```python
import math

import jax
import jax.numpy as jnp
from jax import lax
from jax.sharding import PartitionSpec as P

EXPERTS = 2
BLK = 128


def ring_pairs(n, k):
    return [(i, (i + k) % n) for i in range(n)]


def gather_dp(piece, axis_name):
    n = lax.axis_size(axis_name)
    me = lax.axis_index(axis_name)
    recv = [piece] + [lax.ppermute(piece, axis_name, ring_pairs(n, k)) for k in range(1, n)]
    arr = jnp.stack([recv[(-m) % n] for m in range(n)], axis=1)
    arr2 = jnp.concatenate([arr, arr], axis=1)
    return lax.dynamic_slice_in_dim(arr2, (n - me) % n, n, axis=1)


def scatter_sum_dp(full, axis_name):
    n = lax.axis_size(axis_name)
    me = lax.axis_index(axis_name)
    total = lax.dynamic_index_in_dim(full, me, axis=1, keepdims=False).astype(jnp.float32)
    for k in range(1, n):
        piece = lax.dynamic_index_in_dim(full, (me + k) % n, axis=1, keepdims=False)
        total = total + lax.ppermute(piece, axis_name, ring_pairs(n, k)).astype(jnp.float32)
    return total.astype(jnp.bfloat16)


def local(hidden, combine_weight, down_weight, cotangent, expert_rows, block_expert, slot_token):
    slot_count, hidden_width = hidden.shape
    block_count = block_expert.shape[0]
    n_dp = lax.axis_size("dp")
    positions = jnp.arange(slot_count, dtype=jnp.int32)
    blocks = positions // BLK
    live_rows = expert_rows[0]
    first_blocks = (live_rows[0] + BLK - 1) // BLK
    second_blocks = (live_rows[1] + BLK - 1) // BLK
    live = jnp.where(
        blocks < first_blocks,
        positions < live_rows[0],
        (blocks < first_blocks + second_blocks) & (positions - first_blocks * BLK < live_rows[1]),
    )
    slot_scale = combine_weight * live.astype(jnp.float32)
    slot_expert = jnp.repeat(block_expert, BLK)

    panel = lax.all_gather(jnp.transpose(down_weight, (1, 0, 2)), "fsdp", axis=1, tiled=True)
    model_width = panel.shape[1]

    full_cot = gather_dp(cotangent, "dp").reshape(slot_count, model_width)
    tok_hot = (slot_token[:, None] == positions[None, :]).astype(jnp.bfloat16)
    picked = jnp.dot(tok_hot, full_cot, preferred_element_type=jnp.float32)
    slot_cot = (slot_scale[:, None] * picked).astype(jnp.bfloat16)

    lo = (block_count - 1) * BLK
    masks = [slot_expert == e for e in range(EXPERTS)]
    windows = [(0, lo), (BLK, slot_count)]

    grads = []
    for e in range(EXPERTS):
        a, b = windows[e]
        cot_e = jnp.where(masks[e][a:b, None], slot_cot[a:b], jnp.zeros_like(slot_cot[a:b]))
        grads.append(
            jnp.einsum("sd,sh->dh", cot_e, hidden[a:b], preferred_element_type=jnp.float32).astype(
                jnp.bfloat16
            )
        )
    device_grad = jnp.stack(grads, axis=0)
    summed = lax.psum_scatter(device_grad, "fsdp", scatter_dimension=1, tiled=True).astype(
        jnp.float32
    )
    grad_scale = 1.0 / math.sqrt(lax.axis_size("fsdp") * slot_count)
    grad_down = jnp.transpose((summed * grad_scale).astype(jnp.bfloat16), (1, 0, 2))

    combined = None
    for e in range(EXPERTS):
        valid = live & masks[e]
        target = jnp.where(valid, slot_token, slot_count)
        inv = jnp.zeros((slot_count,), jnp.int32).at[target].set(positions, mode="drop")
        has = jnp.zeros((slot_count,), jnp.bool_).at[target].set(True, mode="drop")
        scale_e = jnp.where(has, slot_scale[inv], 0.0)
        sel = ((inv[:, None] == positions[None, :]) & has[:, None]).astype(jnp.bfloat16)
        hid_e = jnp.dot(sel, hidden, preferred_element_type=jnp.float32).astype(jnp.bfloat16)
        out_e = jnp.einsum("th,dh->td", hid_e, panel[e], preferred_element_type=jnp.float32)
        term = scale_e[:, None] * out_e
        combined = term if combined is None else combined + term
    token_part = combined.astype(jnp.bfloat16).reshape(slot_count, n_dp, model_width // n_dp)
    expert_out = scatter_sum_dp(token_part, "dp")

    gh = []
    for e in range(EXPERTS):
        a, b = windows[e]
        gh.append(jnp.dot(slot_cot[a:b], panel[e], preferred_element_type=jnp.float32))
    head = gh[0][:BLK]
    mid = jnp.where(masks[0][BLK:lo, None], gh[0][BLK:lo], gh[1][: lo - BLK])
    tail = gh[1][lo - BLK :]
    hidden_grad = jnp.concatenate([head, mid, tail], axis=0).astype(jnp.bfloat16)
    return (expert_out, hidden_grad, grad_down)


def solution(mesh):
    in_specs = (
        P("fsdp", "dp"),
        P("fsdp"),
        P("fsdp", None, "dp"),
        P("fsdp", "dp"),
        P("fsdp", None),
        P("fsdp"),
        P("fsdp"),
    )
    out_specs = (P("fsdp", "dp"), P("fsdp", "dp"), P("fsdp", None, "dp"))
    return jax.shard_map(local, mesh=mesh, in_specs=in_specs, out_specs=out_specs, check_vma=False)
```

```python
import math

import jax
import jax.numpy as jnp
from jax import lax
from jax.sharding import PartitionSpec as P

EXPERTS = 2
BLK = 128


def ring_pairs(n, k):
    return [(i, (i + k) % n) for i in range(n)]


def gather_major(piece, axis_name):
    n = lax.axis_size(axis_name)
    me = lax.axis_index(axis_name)
    recv = [piece] + [lax.ppermute(piece, axis_name, ring_pairs(n, k)) for k in range(1, n)]
    arr = jnp.stack([recv[(-m) % n] for m in range(n)] * 2, axis=0)
    return lax.dynamic_slice_in_dim(arr, (n - me) % n, n, axis=0)


def scatter_sum_major(full, axis_name):
    n = lax.axis_size(axis_name)
    me = lax.axis_index(axis_name)
    total = lax.dynamic_index_in_dim(full, me, axis=0, keepdims=False).astype(jnp.float32)
    for k in range(1, n):
        piece = lax.dynamic_index_in_dim(full, (me + k) % n, axis=0, keepdims=False)
        total = total + lax.ppermute(piece, axis_name, ring_pairs(n, k)).astype(jnp.float32)
    return total.astype(jnp.bfloat16)


def local(hidden, combine_weight, down_weight, cotangent, expert_rows, block_expert, slot_token):
    slot_count, hidden_width = hidden.shape
    block_count = block_expert.shape[0]
    n_dp = lax.axis_size("dp")
    part_width = cotangent.shape[1]
    positions = jnp.arange(slot_count, dtype=jnp.int32)
    blocks = positions // BLK
    live_rows = expert_rows[0]
    first_blocks = (live_rows[0] + BLK - 1) // BLK
    second_blocks = (live_rows[1] + BLK - 1) // BLK
    live = jnp.where(
        blocks < first_blocks,
        positions < live_rows[0],
        (blocks < first_blocks + second_blocks) & (positions - first_blocks * BLK < live_rows[1]),
    )
    slot_scale = combine_weight * live.astype(jnp.float32)
    slot_expert = jnp.repeat(block_expert, BLK)

    panel = lax.all_gather(jnp.transpose(down_weight, (1, 0, 2)), "fsdp", axis=1, tiled=True)
    model_width = panel.shape[1]
    panel_parts = panel.reshape(EXPERTS, n_dp, part_width, hidden_width)

    full_cot = gather_major(cotangent, "dp")
    tok_hot = (slot_token[:, None] == positions[None, :]).astype(jnp.bfloat16)
    picked = jnp.einsum("st,jtc->jsc", tok_hot, full_cot, preferred_element_type=jnp.float32)
    slot_cot = (slot_scale[None, :, None] * picked).astype(jnp.bfloat16)

    lo = (block_count - 1) * BLK
    masks = [slot_expert == e for e in range(EXPERTS)]
    windows = [(0, lo), (BLK, slot_count)]

    cot_flat = jnp.transpose(slot_cot, (1, 0, 2)).reshape(slot_count, model_width)
    grads = []
    for e in range(EXPERTS):
        a, b = windows[e]
        cot_w = cot_flat[a:b]
        cot_e = jnp.where(masks[e][a:b, None], cot_w, jnp.zeros_like(cot_w))
        grads.append(
            jnp.einsum("sd,sh->dh", cot_e, hidden[a:b], preferred_element_type=jnp.float32).astype(
                jnp.bfloat16
            )
        )
    device_grad = jnp.stack(grads, axis=0)
    device_grad, panel_parts = lax.optimization_barrier((device_grad, panel_parts))
    summed = lax.psum_scatter(device_grad, "fsdp", scatter_dimension=1, tiled=True).astype(
        jnp.float32
    )
    grad_scale = 1.0 / math.sqrt(lax.axis_size("fsdp") * slot_count)
    grad_down = jnp.transpose((summed * grad_scale).astype(jnp.bfloat16), (1, 0, 2))

    combined = None
    for e in range(EXPERTS):
        valid = live & masks[e]
        target = jnp.where(valid, slot_token, slot_count)
        inv = jnp.zeros((slot_count,), jnp.int32).at[target].set(positions, mode="drop")
        has = jnp.zeros((slot_count,), jnp.bool_).at[target].set(True, mode="drop")
        scale_e = jnp.where(has, slot_scale[inv], 0.0)
        sel = ((inv[:, None] == positions[None, :]) & has[:, None]).astype(jnp.bfloat16)
        hid_e = jnp.dot(sel, hidden, preferred_element_type=jnp.float32).astype(jnp.bfloat16)
        out_e = jnp.einsum("th,jch->jtc", hid_e, panel_parts[e], preferred_element_type=jnp.float32)
        term = scale_e[None, :, None] * out_e
        combined = term if combined is None else combined + term
    expert_out = scatter_sum_major(combined.astype(jnp.bfloat16), "dp")

    gh = []
    for e in range(EXPERTS):
        a, b = windows[e]
        gh.append(
            jnp.einsum(
                "jsc,jch->sh", slot_cot[:, a:b], panel_parts[e], preferred_element_type=jnp.float32
            )
        )
    head = gh[0][:BLK]
    mid = jnp.where(masks[0][BLK:lo, None], gh[0][BLK:lo], gh[1][: lo - BLK])
    tail = gh[1][lo - BLK :]
    hidden_grad = jnp.concatenate([head, mid, tail], axis=0).astype(jnp.bfloat16)
    return (expert_out, hidden_grad, grad_down)


def solution(mesh):
    in_specs = (
        P("fsdp", "dp"),
        P("fsdp"),
        P("fsdp", None, "dp"),
        P("fsdp", "dp"),
        P("fsdp", None),
        P("fsdp"),
        P("fsdp"),
    )
    out_specs = (P("fsdp", "dp"), P("fsdp", "dp"), P("fsdp", None, "dp"))
    return jax.shard_map(local, mesh=mesh, in_specs=in_specs, out_specs=out_specs, check_vma=False)
```

```python
import math

import jax
import jax.numpy as jnp
from jax import lax
from jax.sharding import PartitionSpec as P

EXPERTS = 2
BLK = 128


def ring_pairs(n, k):
    return [(i, (i + k) % n) for i in range(n)]


def gather_major(piece, axis_name):
    n = lax.axis_size(axis_name)
    me = lax.axis_index(axis_name)
    recv = [piece] + [lax.ppermute(piece, axis_name, ring_pairs(n, k)) for k in range(1, n)]
    arr = jnp.stack([recv[(-m) % n] for m in range(n)] * 2, axis=0)
    return lax.dynamic_slice_in_dim(arr, (n - me) % n, n, axis=0)


def scatter_sum_major(full, axis_name):
    n = lax.axis_size(axis_name)
    me = lax.axis_index(axis_name)
    total = lax.dynamic_index_in_dim(full, me, axis=0, keepdims=False).astype(jnp.float32)
    for k in range(1, n):
        piece = lax.dynamic_index_in_dim(full, (me + k) % n, axis=0, keepdims=False)
        total = total + lax.ppermute(piece, axis_name, ring_pairs(n, k)).astype(jnp.float32)
    return total.astype(jnp.bfloat16)


def local(hidden, combine_weight, down_weight, cotangent, expert_rows, block_expert, slot_token):
    slot_count, hidden_width = hidden.shape
    block_count = block_expert.shape[0]
    n_dp = lax.axis_size("dp")
    part_width = cotangent.shape[1]
    positions = jnp.arange(slot_count, dtype=jnp.int32)
    blocks = positions // BLK
    live_rows = expert_rows[0]
    first_blocks = (live_rows[0] + BLK - 1) // BLK
    second_blocks = (live_rows[1] + BLK - 1) // BLK
    live = jnp.where(
        blocks < first_blocks,
        positions < live_rows[0],
        (blocks < first_blocks + second_blocks) & (positions - first_blocks * BLK < live_rows[1]),
    )
    slot_scale = combine_weight * live.astype(jnp.float32)
    slot_expert = jnp.repeat(block_expert, BLK)

    n_core = lax.axis_size("core")
    core = lax.axis_index("core")
    own = lax.all_gather(jnp.transpose(down_weight, (1, 0, 2)), "fo", axis=1, tiled=False)
    other = lax.ppermute(own, "core", ring_pairs(n_core, 1))
    both = jnp.stack([own, other, own], axis=2)
    panel = lax.dynamic_slice_in_dim(both, core, n_core, axis=2)
    model_width = panel.shape[1] * panel.shape[2] * panel.shape[3]
    panel_parts = panel.reshape(EXPERTS, n_dp, model_width // n_dp, hidden_width)

    full_cot = gather_major(cotangent, "dp")
    tok_hot = (slot_token[:, None] == positions[None, :]).astype(jnp.bfloat16)
    picked = jnp.einsum("st,jtc->jsc", tok_hot, full_cot, preferred_element_type=jnp.float32)
    slot_cot = (slot_scale[None, :, None] * picked).astype(jnp.bfloat16)

    lo = (block_count - 1) * BLK
    masks = [slot_expert == e for e in range(EXPERTS)]
    windows = [(0, lo), (BLK, slot_count)]

    cot_flat = jnp.transpose(slot_cot, (1, 0, 2)).reshape(slot_count, model_width)
    grads = []
    for e in range(EXPERTS):
        a, b = windows[e]
        cot_w = cot_flat[a:b]
        cot_e = jnp.where(masks[e][a:b, None], cot_w, jnp.zeros_like(cot_w))
        grads.append(
            jnp.einsum("sd,sh->dh", cot_e, hidden[a:b], preferred_element_type=jnp.float32).astype(
                jnp.bfloat16
            )
        )
    device_grad = jnp.stack(grads, axis=0)
    device_grad, panel_parts = lax.optimization_barrier((device_grad, panel_parts))
    n_fo = lax.axis_size("fo")
    split = device_grad.reshape(EXPERTS, n_fo, n_core, model_width // (n_fo * n_core), hidden_width)
    keep = lax.dynamic_index_in_dim(split, core, axis=2, keepdims=False)
    send = lax.dynamic_index_in_dim(split, (core + 1) % n_core, axis=2, keepdims=False)
    pair_sum = keep.astype(jnp.float32) + lax.ppermute(send, "core", ring_pairs(n_core, 1)).astype(
        jnp.float32
    )
    summed = lax.psum_scatter(pair_sum.astype(jnp.bfloat16), "fo", scatter_dimension=1, tiled=True)
    grad_scale = 1.0 / math.sqrt(lax.axis_size(("fo", "core")) * slot_count)
    summed = summed.reshape(EXPERTS, -1, hidden_width).astype(jnp.float32)
    grad_down = jnp.transpose((summed * grad_scale).astype(jnp.bfloat16), (1, 0, 2))

    combined = None
    for e in range(EXPERTS):
        valid = live & masks[e]
        target = jnp.where(valid, slot_token, slot_count)
        inv = jnp.zeros((slot_count,), jnp.int32).at[target].set(positions, mode="drop")
        has = jnp.zeros((slot_count,), jnp.bool_).at[target].set(True, mode="drop")
        scale_e = jnp.where(has, slot_scale[inv], 0.0)
        sel = ((inv[:, None] == positions[None, :]) & has[:, None]).astype(jnp.bfloat16)
        hid_e = jnp.dot(sel, hidden, preferred_element_type=jnp.float32).astype(jnp.bfloat16)
        out_e = jnp.einsum("th,jch->jtc", hid_e, panel_parts[e], preferred_element_type=jnp.float32)
        term = scale_e[None, :, None] * out_e
        combined = term if combined is None else combined + term
    expert_out = scatter_sum_major(combined.astype(jnp.bfloat16), "dp")

    gh = []
    for e in range(EXPERTS):
        a, b = windows[e]
        gh.append(
            jnp.einsum(
                "jsc,jch->sh", slot_cot[:, a:b], panel_parts[e], preferred_element_type=jnp.float32
            )
        )
    head = gh[0][:BLK]
    mid = jnp.where(masks[0][BLK:lo, None], gh[0][BLK:lo], gh[1][: lo - BLK])
    tail = gh[1][lo - BLK :]
    hidden_grad = jnp.concatenate([head, mid, tail], axis=0).astype(jnp.bfloat16)
    return (expert_out, hidden_grad, grad_down)


def solution(mesh):
    n_fsdp = mesh.shape["fsdp"]
    n_core = 2
    devices = mesh.devices.reshape(n_fsdp // n_core, n_core, mesh.shape["dp"])
    fine = jax.sharding.Mesh(devices, ("fo", "core", "dp"))
    rows = ("fo", "core")
    in_specs = (
        P(rows, "dp"),
        P(rows),
        P(rows, None, "dp"),
        P(rows, "dp"),
        P(rows, None),
        P(rows),
        P(rows),
    )
    out_specs = (P(rows, "dp"), P(rows, "dp"), P(rows, None, "dp"))
    return jax.shard_map(local, mesh=fine, in_specs=in_specs, out_specs=out_specs, check_vma=False)
```

```python
import math

import jax
import jax.numpy as jnp
from jax import lax
from jax.sharding import PartitionSpec as P

EXPERTS = 2
BLK = 128


def ring_pairs(n, k):
    return [(i, (i + k) % n) for i in range(n)]


def in_order(rel, axis_name):
    n = lax.axis_size(axis_name)
    me = lax.axis_index(axis_name)
    arr = jnp.stack(list(rel) * 2, axis=0)
    return lax.dynamic_slice_in_dim(arr, (n - me) % n, n, axis=0)


def ring_gather(x, axis_name):
    n = lax.axis_size(axis_name)
    if n == 2:
        return in_order([x, lax.ppermute(x, axis_name, ring_pairs(n, 1))], axis_name)
    if n == 4:
        half = x.shape[0] // 2
        from_prev = lax.ppermute(x, axis_name, ring_pairs(n, 1))
        from_next = lax.ppermute(x, axis_name, ring_pairs(n, n - 1))
        far_a = lax.ppermute(from_prev[:half], axis_name, ring_pairs(n, 1))
        far_b = lax.ppermute(from_next[half:], axis_name, ring_pairs(n, n - 1))
        far = jnp.concatenate([far_a, far_b], axis=0)
        return in_order([x, from_next, far, from_prev], axis_name)
    recv = [x] + [lax.ppermute(x, axis_name, ring_pairs(n, k)) for k in range(1, n)]
    return in_order([recv[(-m) % n] for m in range(n)], axis_name)


def ring_reduce(blocks, axis_name):
    n = lax.axis_size(axis_name)
    me = lax.axis_index(axis_name)

    def blk(k):
        return lax.dynamic_index_in_dim(blocks, (me + k) % n, axis=0, keepdims=False).astype(jnp.float32)

    def send(v, k):
        return lax.ppermute(v.astype(jnp.bfloat16), axis_name, ring_pairs(n, k)).astype(jnp.float32)

    if n == 4:
        far = blk(2)
        half = far.shape[0] // 2
        got_a = send(far[:half], 1)
        got_b = send(far[half:], n - 1)
        nxt = blk(1)
        prv = blk(n - 1)
        nxt = jnp.concatenate([nxt[:half] + got_a, nxt[half:]], axis=0)
        prv = jnp.concatenate([prv[:half], prv[half:] + got_b], axis=0)
        return blk(0) + send(nxt, 1) + send(prv, n - 1)
    total = blk(0)
    for k in range(1, n):
        total = total + send(blk(k), k)
    return total


def local(hidden, combine_weight, down_weight, cotangent, expert_rows, block_expert, slot_token):
    slot_count, hidden_width = hidden.shape
    block_count = block_expert.shape[0]
    n_dp = lax.axis_size(("z", "xl"))
    part_width = cotangent.shape[1]
    positions = jnp.arange(slot_count, dtype=jnp.int32)
    blocks = positions // BLK
    live_rows = expert_rows[0]
    first_blocks = (live_rows[0] + BLK - 1) // BLK
    second_blocks = (live_rows[1] + BLK - 1) // BLK
    live = jnp.where(
        blocks < first_blocks,
        positions < live_rows[0],
        (blocks < first_blocks + second_blocks) & (positions - first_blocks * BLK < live_rows[1]),
    )
    slot_scale = combine_weight * live.astype(jnp.float32)
    slot_expert = jnp.repeat(block_expert, BLK)

    w = jnp.transpose(down_weight, (1, 0, 2))
    w = ring_gather(w, "xh")
    w = ring_gather(w, "y")
    w = ring_gather(w, "core")
    panel = jnp.transpose(w, (3, 2, 1, 0, 4, 5))
    model_width = panel.shape[1] * panel.shape[2] * panel.shape[3] * panel.shape[4]
    panel_parts = panel.reshape(EXPERTS, n_dp, model_width // n_dp, hidden_width)

    full_cot = ring_gather(ring_gather(cotangent, "xl"), "z").reshape(n_dp, slot_count, part_width)
    tok_hot = (slot_token[:, None] == positions[None, :]).astype(jnp.bfloat16)
    picked = jnp.einsum("st,jtc->jsc", tok_hot, full_cot, preferred_element_type=jnp.float32)
    slot_cot = (slot_scale[None, :, None] * picked).astype(jnp.bfloat16)

    lo = (block_count - 1) * BLK
    masks = [slot_expert == e for e in range(EXPERTS)]
    windows = [(0, lo), (BLK, slot_count)]

    cot_flat = jnp.transpose(slot_cot, (1, 0, 2)).reshape(slot_count, model_width)
    grads = []
    for e in range(EXPERTS):
        a, b = windows[e]
        cot_w = cot_flat[a:b]
        cot_e = jnp.where(masks[e][a:b, None], cot_w, jnp.zeros_like(cot_w))
        grads.append(
            jnp.einsum("sd,sh->dh", cot_e, hidden[a:b], preferred_element_type=jnp.float32).astype(
                jnp.bfloat16
            )
        )
    device_grad = jnp.stack(grads, axis=0)
    fsdp = ("xh", "y", "core")
    summed = lax.psum_scatter(device_grad, fsdp, scatter_dimension=1, tiled=True).astype(jnp.float32)
    grad_scale = 1.0 / math.sqrt(lax.axis_size(fsdp) * slot_count)
    grad_down = jnp.transpose((summed * grad_scale).astype(jnp.bfloat16), (1, 0, 2))

    combined = None
    for e in range(EXPERTS):
        valid = live & masks[e]
        target = jnp.where(valid, slot_token, slot_count)
        inv = jnp.zeros((slot_count,), jnp.int32).at[target].set(positions, mode="drop")
        has = jnp.zeros((slot_count,), jnp.bool_).at[target].set(True, mode="drop")
        scale_e = jnp.where(has, slot_scale[inv], 0.0)
        sel = ((inv[:, None] == positions[None, :]) & has[:, None]).astype(jnp.bfloat16)
        hid_e = jnp.dot(sel, hidden, preferred_element_type=jnp.float32).astype(jnp.bfloat16)
        out_e = jnp.einsum("th,jch->jtc", hid_e, panel_parts[e], preferred_element_type=jnp.float32)
        term = scale_e[None, :, None] * out_e
        combined = term if combined is None else combined + term
    token_part = combined.astype(jnp.bfloat16)
    n_xl = lax.axis_size("xl")
    by_z = ring_reduce(token_part.reshape(n_dp // n_xl, n_xl, slot_count, part_width), "z")
    expert_out = ring_reduce(by_z, "xl").astype(jnp.bfloat16)

    gh = []
    for e in range(EXPERTS):
        a, b = windows[e]
        gh.append(
            jnp.einsum(
                "jsc,jch->sh", slot_cot[:, a:b], panel_parts[e], preferred_element_type=jnp.float32
            )
        )
    head = gh[0][:BLK]
    mid = jnp.where(masks[0][BLK:lo, None], gh[0][BLK:lo], gh[1][: lo - BLK])
    tail = gh[1][lo - BLK :]
    hidden_grad = jnp.concatenate([head, mid, tail], axis=0).astype(jnp.bfloat16)
    return (expert_out, hidden_grad, grad_down)


def solution(mesh):
    n_core = 2
    n_fsdp = mesh.shape["fsdp"]
    n_dp = mesh.shape["dp"]
    n_x = 2
    shape = (n_x, n_fsdp // (n_x * n_core), n_core, n_dp // n_x, n_x)
    fine = jax.sharding.Mesh(mesh.devices.reshape(shape), ("xh", "y", "core", "z", "xl"))
    rows = ("xh", "y", "core")
    cols = ("z", "xl")
    in_specs = (
        P(rows, cols),
        P(rows),
        P(rows, None, cols),
        P(rows, cols),
        P(rows, None),
        P(rows),
        P(rows),
    )
    out_specs = (P(rows, cols), P(rows, cols), P(rows, None, cols))
    return jax.shard_map(local, mesh=fine, in_specs=in_specs, out_specs=out_specs, check_vma=False)
```

```python
import math

import jax
import jax.numpy as jnp
from jax import lax
from jax.sharding import PartitionSpec as P

EXPERTS = 2
BLK = 128


def ring_pairs(n, k):
    return [(i, (i + k) % n) for i in range(n)]


def in_order(rel, axis_name):
    n = lax.axis_size(axis_name)
    me = lax.axis_index(axis_name)
    arr = jnp.stack(list(rel) * 2, axis=0)
    return lax.dynamic_slice_in_dim(arr, (n - me) % n, n, axis=0)


def ring_parts(x, axis_name):
    n = lax.axis_size(axis_name)
    if n == 4:
        half = x.shape[0] // 2
        from_prev = lax.ppermute(x, axis_name, ring_pairs(n, 1))
        from_next = lax.ppermute(x, axis_name, ring_pairs(n, n - 1))
        far_a = lax.ppermute(from_prev[:half], axis_name, ring_pairs(n, 1))
        far_b = lax.ppermute(from_next[half:], axis_name, ring_pairs(n, n - 1))
        far = jnp.concatenate([far_a, far_b], axis=0)
        return [x, from_next, far, from_prev]
    recv = [x] + [lax.ppermute(x, axis_name, ring_pairs(n, k)) for k in range(1, n)]
    return [recv[(-m) % n] for m in range(n)]


def ring_gather(x, axis_name):
    return in_order(ring_parts(x, axis_name), axis_name)


def ring_reduce(blocks, axis_name):
    n = lax.axis_size(axis_name)
    me = lax.axis_index(axis_name)

    def blk(k):
        return lax.dynamic_index_in_dim(blocks, (me + k) % n, axis=0, keepdims=False).astype(jnp.float32)

    def send(v, k):
        return lax.ppermute(v.astype(jnp.bfloat16), axis_name, ring_pairs(n, k)).astype(jnp.float32)

    if n == 4:
        far = blk(2)
        half = far.shape[0] // 2
        got_a = send(far[:half], 1)
        got_b = send(far[half:], n - 1)
        nxt = blk(1)
        prv = blk(n - 1)
        nxt = jnp.concatenate([nxt[:half] + got_a, nxt[half:]], axis=0)
        prv = jnp.concatenate([prv[:half], prv[half:] + got_b], axis=0)
        return blk(0) + send(nxt, 1) + send(prv, n - 1)
    total = blk(0)
    for k in range(1, n):
        total = total + send(blk(k), k)
    return total


def local(hidden, combine_weight, down_weight, cotangent, expert_rows, block_expert, slot_token):
    slot_count, hidden_width = hidden.shape
    block_count = block_expert.shape[0]
    n_dp = lax.axis_size(("z", "xl"))
    part_width = cotangent.shape[1]
    positions = jnp.arange(slot_count, dtype=jnp.int32)
    blocks = positions // BLK
    live_rows = expert_rows[0]
    first_blocks = (live_rows[0] + BLK - 1) // BLK
    second_blocks = (live_rows[1] + BLK - 1) // BLK
    live = jnp.where(
        blocks < first_blocks,
        positions < live_rows[0],
        (blocks < first_blocks + second_blocks) & (positions - first_blocks * BLK < live_rows[1]),
    )
    slot_scale = combine_weight * live.astype(jnp.float32)
    slot_expert = jnp.repeat(block_expert, BLK)

    n_xh, n_y, n_core = lax.axis_size("xh"), lax.axis_size("y"), lax.axis_size("core")
    xh, y, core = lax.axis_index("xh"), lax.axis_index("y"), lax.axis_index("core")
    w = jnp.transpose(down_weight, (1, 0, 2))
    pair = jnp.stack([w, lax.ppermute(w, "xh", ring_pairs(n_xh, 1))], axis=0)
    ring = ring_parts(pair, "y")
    quad = jnp.stack(ring, axis=0)
    both = [quad, lax.ppermute(quad, "core", ring_pairs(n_core, 1))]
    panel = jnp.zeros((EXPERTS, n_xh * n_y * n_core) + w.shape[1:], w.dtype)
    for c in range(n_core):
        for m in range(len(ring)):
            for a in range(2):
                f = ((xh + a) % n_xh * n_y + (y + m) % n_y) * n_core + (core + c) % n_core
                piece = both[c][m, a][:, None]
                panel = lax.dynamic_update_slice(panel, piece, (0, f, 0, 0))
    model_width = panel.shape[1] * panel.shape[2]
    panel_parts = panel.reshape(EXPERTS, n_dp, model_width // n_dp, hidden_width)

    full_cot = ring_gather(ring_gather(cotangent, "xl"), "z").reshape(n_dp, slot_count, part_width)
    tok_hot = (slot_token[:, None] == positions[None, :]).astype(jnp.bfloat16)
    picked = jnp.einsum("st,jtc->jsc", tok_hot, full_cot, preferred_element_type=jnp.float32)
    slot_cot = (slot_scale[None, :, None] * picked).astype(jnp.bfloat16)

    lo = (block_count - 1) * BLK
    masks = [slot_expert == e for e in range(EXPERTS)]
    windows = [(0, lo), (BLK, slot_count)]

    cot_flat = jnp.transpose(slot_cot, (1, 0, 2)).reshape(slot_count, model_width)
    grads = []
    for e in range(EXPERTS):
        a, b = windows[e]
        cot_w = cot_flat[a:b]
        cot_e = jnp.where(masks[e][a:b, None], cot_w, jnp.zeros_like(cot_w))
        grads.append(
            jnp.einsum("sd,sh->dh", cot_e, hidden[a:b], preferred_element_type=jnp.float32).astype(
                jnp.bfloat16
            )
        )
    device_grad = jnp.stack(grads, axis=0)
    fsdp = ("xh", "y", "core")
    summed = lax.psum_scatter(device_grad, fsdp, scatter_dimension=1, tiled=True).astype(jnp.float32)
    grad_scale = 1.0 / math.sqrt(lax.axis_size(fsdp) * slot_count)
    grad_down = jnp.transpose((summed * grad_scale).astype(jnp.bfloat16), (1, 0, 2))

    combined = None
    for e in range(EXPERTS):
        valid = live & masks[e]
        target = jnp.where(valid, slot_token, slot_count)
        inv = jnp.zeros((slot_count,), jnp.int32).at[target].set(positions, mode="drop")
        has = jnp.zeros((slot_count,), jnp.bool_).at[target].set(True, mode="drop")
        scale_e = jnp.where(has, slot_scale[inv], 0.0)
        sel = ((inv[:, None] == positions[None, :]) & has[:, None]).astype(jnp.bfloat16)
        hid_e = jnp.dot(sel, hidden, preferred_element_type=jnp.float32).astype(jnp.bfloat16)
        out_e = jnp.einsum("th,jch->jtc", hid_e, panel_parts[e], preferred_element_type=jnp.float32)
        term = scale_e[None, :, None] * out_e
        combined = term if combined is None else combined + term
    token_part = combined.astype(jnp.bfloat16)
    n_xl = lax.axis_size("xl")
    by_z = ring_reduce(token_part.reshape(n_dp // n_xl, n_xl, slot_count, part_width), "z")
    expert_out = ring_reduce(by_z, "xl").astype(jnp.bfloat16)

    gh = []
    for e in range(EXPERTS):
        a, b = windows[e]
        gh.append(
            jnp.einsum(
                "jsc,jch->sh", slot_cot[:, a:b], panel_parts[e], preferred_element_type=jnp.float32
            )
        )
    head = gh[0][:BLK]
    mid = jnp.where(masks[0][BLK:lo, None], gh[0][BLK:lo], gh[1][: lo - BLK])
    tail = gh[1][lo - BLK :]
    hidden_grad = jnp.concatenate([head, mid, tail], axis=0).astype(jnp.bfloat16)
    return (expert_out, hidden_grad, grad_down)


def solution(mesh):
    n_core = 2
    n_fsdp = mesh.shape["fsdp"]
    n_dp = mesh.shape["dp"]
    n_x = 2
    shape = (n_x, n_fsdp // (n_x * n_core), n_core, n_dp // n_x, n_x)
    fine = jax.sharding.Mesh(mesh.devices.reshape(shape), ("xh", "y", "core", "z", "xl"))
    rows = ("xh", "y", "core")
    cols = ("z", "xl")
    in_specs = (
        P(rows, cols),
        P(rows),
        P(rows, None, cols),
        P(rows, cols),
        P(rows, None),
        P(rows),
        P(rows),
    )
    out_specs = (P(rows, cols), P(rows, cols), P(rows, None, cols))
    return jax.shard_map(local, mesh=fine, in_specs=in_specs, out_specs=out_specs, check_vma=False)
```

```python
import math

import jax
import jax.numpy as jnp
from jax import lax
from jax.sharding import PartitionSpec as P

EXPERTS = 2
BLK = 128


def ring_pairs(n, k):
    return [(i, (i + k) % n) for i in range(n)]


def in_order(rel, axis_name):
    n = lax.axis_size(axis_name)
    me = lax.axis_index(axis_name)
    arr = jnp.stack(list(rel) * 2, axis=0)
    return lax.dynamic_slice_in_dim(arr, (n - me) % n, n, axis=0)


def ring_parts(x, axis_name):
    n = lax.axis_size(axis_name)
    if n == 4:
        half = x.shape[0] // 2
        from_prev = lax.ppermute(x, axis_name, ring_pairs(n, 1))
        from_next = lax.ppermute(x, axis_name, ring_pairs(n, n - 1))
        far_a = lax.ppermute(from_prev[:half], axis_name, ring_pairs(n, 1))
        far_b = lax.ppermute(from_next[half:], axis_name, ring_pairs(n, n - 1))
        far = jnp.concatenate([far_a, far_b], axis=0)
        return [x, from_next, far, from_prev]
    recv = [x] + [lax.ppermute(x, axis_name, ring_pairs(n, k)) for k in range(1, n)]
    return [recv[(-m) % n] for m in range(n)]


def ring_gather(x, axis_name):
    return in_order(ring_parts(x, axis_name), axis_name)


def ring_reduce(blocks, axis_name):
    n = lax.axis_size(axis_name)
    me = lax.axis_index(axis_name)

    def blk(k):
        return lax.dynamic_index_in_dim(blocks, (me + k) % n, axis=0, keepdims=False).astype(jnp.float32)

    def send(v, k):
        return lax.ppermute(v.astype(jnp.bfloat16), axis_name, ring_pairs(n, k)).astype(jnp.float32)

    if n == 4:
        far = blk(2)
        half = far.shape[0] // 2
        got_a = send(far[:half], 1)
        got_b = send(far[half:], n - 1)
        nxt = blk(1)
        prv = blk(n - 1)
        nxt = jnp.concatenate([nxt[:half] + got_a, nxt[half:]], axis=0)
        prv = jnp.concatenate([prv[:half], prv[half:] + got_b], axis=0)
        return blk(0) + send(nxt, 1) + send(prv, n - 1)
    total = blk(0)
    for k in range(1, n):
        total = total + send(blk(k), k)
    return total


def local(hidden, combine_weight, down_weight, cotangent, expert_rows, block_expert, slot_token):
    slot_count, hidden_width = hidden.shape
    block_count = block_expert.shape[0]
    n_dp = lax.axis_size(("z", "xl"))
    part_width = cotangent.shape[1]
    positions = jnp.arange(slot_count, dtype=jnp.int32)
    blocks = positions // BLK
    live_rows = expert_rows[0]
    first_blocks = (live_rows[0] + BLK - 1) // BLK
    second_blocks = (live_rows[1] + BLK - 1) // BLK
    live = jnp.where(
        blocks < first_blocks,
        positions < live_rows[0],
        (blocks < first_blocks + second_blocks) & (positions - first_blocks * BLK < live_rows[1]),
    )
    slot_scale = combine_weight * live.astype(jnp.float32)
    slot_expert = jnp.repeat(block_expert, BLK)

    n_xh, n_y, n_core = lax.axis_size("xh"), lax.axis_size("y"), lax.axis_size("core")
    xh, y, core = lax.axis_index("xh"), lax.axis_index("y"), lax.axis_index("core")
    w = down_weight.reshape(down_weight.shape[0], EXPERTS * hidden_width)
    pair = jnp.stack([w, lax.ppermute(w, "xh", ring_pairs(n_xh, 1))], axis=0)
    ring = ring_parts(pair, "y")
    quad = jnp.stack(ring, axis=0)
    both = [quad, lax.ppermute(quad, "core", ring_pairs(n_core, 1))]
    panel = jnp.zeros((n_xh * n_y * n_core,) + w.shape, w.dtype)
    for c in range(n_core):
        for m in range(len(ring)):
            for a in range(2):
                f = ((xh + a) % n_xh * n_y + (y + m) % n_y) * n_core + (core + c) % n_core
                panel = lax.dynamic_update_slice(panel, both[c][m, a][None], (f, 0, 0))
    model_width = panel.shape[0] * panel.shape[1]
    panel = panel.reshape(model_width, EXPERTS, hidden_width)
    panel_e = [panel[:, e, :] for e in range(EXPERTS)]
    panel_parts = [p.reshape(n_dp, model_width // n_dp, hidden_width) for p in panel_e]

    full_cot = ring_gather(ring_gather(cotangent, "xl"), "z").reshape(n_dp, slot_count, part_width)
    tok_hot = (slot_token[:, None] == positions[None, :]).astype(jnp.bfloat16)
    picked = jnp.einsum("st,jtc->sjc", tok_hot, full_cot, preferred_element_type=jnp.float32)
    slot_cot = (slot_scale[:, None] * picked.reshape(slot_count, model_width)).astype(jnp.bfloat16)

    lo = (block_count - 1) * BLK
    masks = [slot_expert == e for e in range(EXPERTS)]
    windows = [(0, lo), (BLK, slot_count)]

    cot_flat = slot_cot
    grads = []
    for e in range(EXPERTS):
        a, b = windows[e]
        cot_w = cot_flat[a:b]
        cot_e = jnp.where(masks[e][a:b, None], cot_w, jnp.zeros_like(cot_w))
        grads.append(
            jnp.einsum("sd,sh->dh", cot_e, hidden[a:b], preferred_element_type=jnp.float32).astype(
                jnp.bfloat16
            )
        )
    device_grad = jnp.stack(grads, axis=0)
    fsdp = ("xh", "y", "core")
    summed = lax.psum_scatter(device_grad, fsdp, scatter_dimension=1, tiled=True).astype(jnp.float32)
    grad_scale = 1.0 / math.sqrt(lax.axis_size(fsdp) * slot_count)
    grad_down = jnp.transpose((summed * grad_scale).astype(jnp.bfloat16), (1, 0, 2))

    combined = None
    for e in range(EXPERTS):
        valid = live & masks[e]
        target = jnp.where(valid, slot_token, slot_count)
        inv = jnp.zeros((slot_count,), jnp.int32).at[target].set(positions, mode="drop")
        has = jnp.zeros((slot_count,), jnp.bool_).at[target].set(True, mode="drop")
        scale_e = jnp.where(has, slot_scale[inv], 0.0)
        sel = ((inv[:, None] == positions[None, :]) & has[:, None]).astype(jnp.bfloat16)
        hid_e = jnp.dot(sel, hidden, preferred_element_type=jnp.float32).astype(jnp.bfloat16)
        out_e = jnp.einsum("th,jch->jtc", hid_e, panel_parts[e], preferred_element_type=jnp.float32)
        term = scale_e[None, :, None] * out_e
        combined = term if combined is None else combined + term
    token_part = combined.astype(jnp.bfloat16)
    n_xl = lax.axis_size("xl")
    by_z = ring_reduce(token_part.reshape(n_dp // n_xl, n_xl, slot_count, part_width), "z")
    expert_out = ring_reduce(by_z, "xl").astype(jnp.bfloat16)

    gh = []
    for e in range(EXPERTS):
        a, b = windows[e]
        gh.append(jnp.dot(slot_cot[a:b], panel_e[e], preferred_element_type=jnp.float32))
    head = gh[0][:BLK]
    mid = jnp.where(masks[0][BLK:lo, None], gh[0][BLK:lo], gh[1][: lo - BLK])
    tail = gh[1][lo - BLK :]
    hidden_grad = jnp.concatenate([head, mid, tail], axis=0).astype(jnp.bfloat16)
    return (expert_out, hidden_grad, grad_down)


def solution(mesh):
    n_core = 2
    n_fsdp = mesh.shape["fsdp"]
    n_dp = mesh.shape["dp"]
    n_x = 2
    shape = (n_x, n_fsdp // (n_x * n_core), n_core, n_dp // n_x, n_x)
    fine = jax.sharding.Mesh(mesh.devices.reshape(shape), ("xh", "y", "core", "z", "xl"))
    rows = ("xh", "y", "core")
    cols = ("z", "xl")
    in_specs = (
        P(rows, cols),
        P(rows),
        P(rows, None, cols),
        P(rows, cols),
        P(rows, None),
        P(rows),
        P(rows),
    )
    out_specs = (P(rows, cols), P(rows, cols), P(rows, None, cols))
    return jax.shard_map(local, mesh=fine, in_specs=in_specs, out_specs=out_specs, check_vma=False)
```

```python
import math

import jax
import jax.numpy as jnp
from jax import lax
from jax.sharding import PartitionSpec as P

EXPERTS = 2
BLK = 128


def ring_pairs(n, k):
    return [(i, (i + k) % n) for i in range(n)]


def in_order(rel, axis_name):
    n = lax.axis_size(axis_name)
    me = lax.axis_index(axis_name)
    arr = jnp.stack(list(rel) * 2, axis=0)
    return lax.dynamic_slice_in_dim(arr, (n - me) % n, n, axis=0)


def ring_parts(x, axis_name):
    n = lax.axis_size(axis_name)
    if n == 4:
        half = x.shape[0] // 2
        from_prev = lax.ppermute(x, axis_name, ring_pairs(n, 1))
        from_next = lax.ppermute(x, axis_name, ring_pairs(n, n - 1))
        far_a = lax.ppermute(from_prev[:half], axis_name, ring_pairs(n, 1))
        far_b = lax.ppermute(from_next[half:], axis_name, ring_pairs(n, n - 1))
        far = jnp.concatenate([far_a, far_b], axis=0)
        return [x, from_next, far, from_prev]
    recv = [x] + [lax.ppermute(x, axis_name, ring_pairs(n, k)) for k in range(1, n)]
    return [recv[(-m) % n] for m in range(n)]


def ring_gather(x, axis_name):
    return in_order(ring_parts(x, axis_name), axis_name)


def ring_reduce(blocks, axis_name):
    n = lax.axis_size(axis_name)
    me = lax.axis_index(axis_name)

    def blk(k):
        return lax.dynamic_index_in_dim(blocks, (me + k) % n, axis=0, keepdims=False).astype(jnp.float32)

    def send(v, k):
        return lax.ppermute(v.astype(jnp.bfloat16), axis_name, ring_pairs(n, k)).astype(jnp.float32)

    if n == 4:
        far = blk(2)
        half = far.shape[0] // 2
        got_a = send(far[:half], 1)
        got_b = send(far[half:], n - 1)
        nxt = blk(1)
        prv = blk(n - 1)
        nxt = jnp.concatenate([nxt[:half] + got_a, nxt[half:]], axis=0)
        prv = jnp.concatenate([prv[:half], prv[half:] + got_b], axis=0)
        return blk(0) + send(nxt, 1) + send(prv, n - 1)
    total = blk(0)
    for k in range(1, n):
        total = total + send(blk(k), k)
    return total


def local(hidden, combine_weight, down_weight, cotangent, expert_rows, block_expert, slot_token):
    slot_count, hidden_width = hidden.shape
    block_count = block_expert.shape[0]
    n_dp = lax.axis_size(("z", "xl"))
    part_width = cotangent.shape[1]
    positions = jnp.arange(slot_count, dtype=jnp.int32)
    blocks = positions // BLK
    live_rows = expert_rows[0]
    first_blocks = (live_rows[0] + BLK - 1) // BLK
    second_blocks = (live_rows[1] + BLK - 1) // BLK
    live = jnp.where(
        blocks < first_blocks,
        positions < live_rows[0],
        (blocks < first_blocks + second_blocks) & (positions - first_blocks * BLK < live_rows[1]),
    )
    slot_scale = combine_weight * live.astype(jnp.float32)
    slot_expert = jnp.repeat(block_expert, BLK)

    fsdp = ("xh", "y", "core")
    w = down_weight.reshape(down_weight.shape[0], EXPERTS * hidden_width)
    panel = lax.all_gather(w, fsdp, axis=0, tiled=True)
    model_width = panel.shape[0]
    panel_e = [panel[:, e * hidden_width : (e + 1) * hidden_width] for e in range(EXPERTS)]
    panel_parts = [p.reshape(n_dp, model_width // n_dp, hidden_width) for p in panel_e]

    full_cot = ring_gather(ring_gather(cotangent, "xl"), "z").reshape(n_dp, slot_count, part_width)
    tok_hot = (slot_token[:, None] == positions[None, :]).astype(jnp.bfloat16)
    picked = jnp.einsum("st,jtc->sjc", tok_hot, full_cot, preferred_element_type=jnp.float32)
    slot_cot = (slot_scale[:, None] * picked.reshape(slot_count, model_width)).astype(jnp.bfloat16)

    lo = (block_count - 1) * BLK
    masks = [slot_expert == e for e in range(EXPERTS)]
    windows = [(0, lo), (BLK, slot_count)]

    cot_flat = slot_cot
    grads = []
    for e in range(EXPERTS):
        a, b = windows[e]
        cot_w = cot_flat[a:b]
        cot_e = jnp.where(masks[e][a:b, None], cot_w, jnp.zeros_like(cot_w))
        grads.append(
            jnp.einsum("sd,sh->dh", cot_e, hidden[a:b], preferred_element_type=jnp.float32).astype(
                jnp.bfloat16
            )
        )
    device_grad = jnp.stack(grads, axis=0)
    device_grad, panel = lax.optimization_barrier((device_grad, panel))
    summed = lax.psum_scatter(device_grad, fsdp, scatter_dimension=1, tiled=True).astype(jnp.float32)
    grad_scale = 1.0 / math.sqrt(lax.axis_size(fsdp) * slot_count)
    grad_down = jnp.transpose((summed * grad_scale).astype(jnp.bfloat16), (1, 0, 2))

    combined = None
    for e in range(EXPERTS):
        valid = live & masks[e]
        target = jnp.where(valid, slot_token, slot_count)
        inv = jnp.zeros((slot_count,), jnp.int32).at[target].set(positions, mode="drop")
        has = jnp.zeros((slot_count,), jnp.bool_).at[target].set(True, mode="drop")
        scale_e = jnp.where(has, slot_scale[inv], 0.0)
        sel = ((inv[:, None] == positions[None, :]) & has[:, None]).astype(jnp.bfloat16)
        hid_e = jnp.dot(sel, hidden, preferred_element_type=jnp.float32).astype(jnp.bfloat16)
        out_e = jnp.einsum("th,jch->jtc", hid_e, panel_parts[e], preferred_element_type=jnp.float32)
        term = scale_e[None, :, None] * out_e
        combined = term if combined is None else combined + term
    token_part = combined.astype(jnp.bfloat16)
    n_xl = lax.axis_size("xl")
    by_z = ring_reduce(token_part.reshape(n_dp // n_xl, n_xl, slot_count, part_width), "z")
    expert_out = ring_reduce(by_z, "xl").astype(jnp.bfloat16)

    both = jnp.dot(slot_cot, panel, preferred_element_type=jnp.float32)
    hidden_grad = jnp.where(
        masks[0][:, None], both[:, :hidden_width], both[:, hidden_width:]
    ).astype(jnp.bfloat16)
    return (expert_out, hidden_grad, grad_down)


def solution(mesh):
    n_core = 2
    n_fsdp = mesh.shape["fsdp"]
    n_dp = mesh.shape["dp"]
    n_x = 2
    shape = (n_x, n_fsdp // (n_x * n_core), n_core, n_dp // n_x, n_x)
    fine = jax.sharding.Mesh(mesh.devices.reshape(shape), ("xh", "y", "core", "z", "xl"))
    rows = ("xh", "y", "core")
    cols = ("z", "xl")
    in_specs = (
        P(rows, cols),
        P(rows),
        P(rows, None, cols),
        P(rows, cols),
        P(rows, None),
        P(rows),
        P(rows),
    )
    out_specs = (P(rows, cols), P(rows, cols), P(rows, None, cols))
    return jax.shard_map(local, mesh=fine, in_specs=in_specs, out_specs=out_specs, check_vma=False)
```

```python
import math

import jax
import jax.numpy as jnp
from jax import lax
from jax.sharding import PartitionSpec as P

EXPERTS = 2
BLK = 128


def ring_pairs(n, k):
    return [(i, (i + k) % n) for i in range(n)]


def in_order(rel, axis_name):
    n = lax.axis_size(axis_name)
    me = lax.axis_index(axis_name)
    arr = jnp.stack(list(rel) * 2, axis=0)
    return lax.dynamic_slice_in_dim(arr, (n - me) % n, n, axis=0)


def ring_parts(x, axis_name):
    n = lax.axis_size(axis_name)
    if n == 4:
        half = x.shape[0] // 2
        from_prev = lax.ppermute(x, axis_name, ring_pairs(n, 1))
        from_next = lax.ppermute(x, axis_name, ring_pairs(n, n - 1))
        far_a = lax.ppermute(from_prev[:half], axis_name, ring_pairs(n, 1))
        far_b = lax.ppermute(from_next[half:], axis_name, ring_pairs(n, n - 1))
        far = jnp.concatenate([far_a, far_b], axis=0)
        return [x, from_next, far, from_prev]
    recv = [x] + [lax.ppermute(x, axis_name, ring_pairs(n, k)) for k in range(1, n)]
    return [recv[(-m) % n] for m in range(n)]


def ring_gather(x, axis_name):
    return in_order(ring_parts(x, axis_name), axis_name)


def ring_reduce(blocks, axis_name):
    n = lax.axis_size(axis_name)
    me = lax.axis_index(axis_name)

    def blk(k):
        return lax.dynamic_index_in_dim(blocks, (me + k) % n, axis=0, keepdims=False).astype(jnp.float32)

    def send(v, k):
        return lax.ppermute(v.astype(jnp.bfloat16), axis_name, ring_pairs(n, k)).astype(jnp.float32)

    if n == 4:
        far = blk(2)
        half = far.shape[0] // 2
        got_a = send(far[:half], 1)
        got_b = send(far[half:], n - 1)
        nxt = blk(1)
        prv = blk(n - 1)
        nxt = jnp.concatenate([nxt[:half] + got_a, nxt[half:]], axis=0)
        prv = jnp.concatenate([prv[:half], prv[half:] + got_b], axis=0)
        return blk(0) + send(nxt, 1) + send(prv, n - 1)
    total = blk(0)
    for k in range(1, n):
        total = total + send(blk(k), k)
    return total


def local(hidden, combine_weight, down_weight, cotangent, expert_rows, block_expert, slot_token):
    slot_count, hidden_width = hidden.shape
    block_count = block_expert.shape[0]
    n_dp = lax.axis_size(("z", "xl"))
    part_width = cotangent.shape[1]
    positions = jnp.arange(slot_count, dtype=jnp.int32)
    blocks = positions // BLK
    live_rows = expert_rows[0]
    first_blocks = (live_rows[0] + BLK - 1) // BLK
    second_blocks = (live_rows[1] + BLK - 1) // BLK
    live = jnp.where(
        blocks < first_blocks,
        positions < live_rows[0],
        (blocks < first_blocks + second_blocks) & (positions - first_blocks * BLK < live_rows[1]),
    )
    slot_scale = combine_weight * live.astype(jnp.float32)
    slot_expert = jnp.repeat(block_expert, BLK)

    fsdp = ("xh", "y", "core")
    w = down_weight.reshape(down_weight.shape[0], EXPERTS * hidden_width)
    panel = lax.all_gather(w, fsdp, axis=0, tiled=True)
    model_width = panel.shape[0]
    panel_e = [panel[:, e * hidden_width : (e + 1) * hidden_width] for e in range(EXPERTS)]
    panel_parts = [p.reshape(n_dp, model_width // n_dp, hidden_width) for p in panel_e]

    prep = []
    for e in range(EXPERTS):
        valid = live & (slot_expert == e)
        target = jnp.where(valid, slot_token, slot_count)
        inv = jnp.zeros((slot_count,), jnp.int32).at[target].set(positions, mode="drop")
        has = jnp.zeros((slot_count,), jnp.bool_).at[target].set(True, mode="drop")
        scale_e = jnp.where(has, slot_scale[inv], 0.0)
        sel = ((inv[:, None] == positions[None, :]) & has[:, None]).astype(jnp.bfloat16)
        hid_e = jnp.dot(sel, hidden, preferred_element_type=jnp.float32).astype(jnp.bfloat16)
        prep.append((scale_e, hid_e))

    pair = ring_gather(cotangent, "xl")
    parts = ring_parts(pair, "z")
    prep, far = lax.optimization_barrier((prep, parts[2]))
    parts[2] = far
    tok_hot = (slot_token[:, None] == positions[None, :]).astype(jnp.bfloat16)
    picked = [
        jnp.einsum("st,xtc->sxc", tok_hot, p, preferred_element_type=jnp.float32) for p in parts
    ]
    rel = [(slot_scale[:, None, None] * p).astype(jnp.bfloat16) for p in picked]
    n_z = lax.axis_size("z")
    z = lax.axis_index("z")
    rel2 = jnp.stack(rel * 2, axis=1)
    slot_cot = lax.dynamic_slice_in_dim(rel2, (n_z - z) % n_z, n_z, axis=1).reshape(
        slot_count, model_width
    )

    lo = (block_count - 1) * BLK
    masks = [slot_expert == e for e in range(EXPERTS)]
    windows = [(0, lo), (BLK, slot_count)]

    cot_flat = slot_cot
    grads = []
    for e in range(EXPERTS):
        a, b = windows[e]
        cot_w = cot_flat[a:b]
        cot_e = jnp.where(masks[e][a:b, None], cot_w, jnp.zeros_like(cot_w))
        grads.append(
            jnp.einsum("sd,sh->dh", cot_e, hidden[a:b], preferred_element_type=jnp.float32).astype(
                jnp.bfloat16
            )
        )
    device_grad = jnp.stack(grads, axis=0)
    device_grad, panel = lax.optimization_barrier((device_grad, panel))
    summed = lax.psum_scatter(device_grad, fsdp, scatter_dimension=1, tiled=True).astype(jnp.float32)
    grad_scale = 1.0 / math.sqrt(lax.axis_size(fsdp) * slot_count)
    grad_down = jnp.transpose((summed * grad_scale).astype(jnp.bfloat16), (1, 0, 2))

    combined = None
    for e in range(EXPERTS):
        scale_e, hid_e = prep[e]
        out_e = jnp.einsum("th,jch->jtc", hid_e, panel_parts[e], preferred_element_type=jnp.float32)
        term = scale_e[None, :, None] * out_e
        combined = term if combined is None else combined + term
    token_part = combined.astype(jnp.bfloat16)
    n_xl = lax.axis_size("xl")
    by_z = ring_reduce(token_part.reshape(n_dp // n_xl, n_xl, slot_count, part_width), "z")
    expert_out = ring_reduce(by_z, "xl").astype(jnp.bfloat16)

    both = jnp.dot(slot_cot, panel, preferred_element_type=jnp.float32)
    hidden_grad = jnp.where(
        masks[0][:, None], both[:, :hidden_width], both[:, hidden_width:]
    ).astype(jnp.bfloat16)
    return (expert_out, hidden_grad, grad_down)


def solution(mesh):
    n_core = 2
    n_fsdp = mesh.shape["fsdp"]
    n_dp = mesh.shape["dp"]
    n_x = 2
    shape = (n_x, n_fsdp // (n_x * n_core), n_core, n_dp // n_x, n_x)
    fine = jax.sharding.Mesh(mesh.devices.reshape(shape), ("xh", "y", "core", "z", "xl"))
    rows = ("xh", "y", "core")
    cols = ("z", "xl")
    in_specs = (
        P(rows, cols),
        P(rows),
        P(rows, None, cols),
        P(rows, cols),
        P(rows, None),
        P(rows),
        P(rows),
    )
    out_specs = (P(rows, cols), P(rows, cols), P(rows, None, cols))
    return jax.shard_map(local, mesh=fine, in_specs=in_specs, out_specs=out_specs, check_vma=False)
```

```python
import math

import jax
import jax.numpy as jnp
from jax import lax
from jax.sharding import PartitionSpec as P

EXPERTS = 2
BLK = 128


def ring_pairs(n, k):
    return [(i, (i + k) % n) for i in range(n)]


def in_order(rel, axis_name):
    n = lax.axis_size(axis_name)
    me = lax.axis_index(axis_name)
    arr = jnp.stack(list(rel) * 2, axis=0)
    return lax.dynamic_slice_in_dim(arr, (n - me) % n, n, axis=0)


def ring_parts(x, axis_name):
    n = lax.axis_size(axis_name)
    if n == 4:
        half = x.shape[0] // 2
        from_prev = lax.ppermute(x, axis_name, ring_pairs(n, 1))
        from_next = lax.ppermute(x, axis_name, ring_pairs(n, n - 1))
        far_a = lax.ppermute(from_prev[:half], axis_name, ring_pairs(n, 1))
        far_b = lax.ppermute(from_next[half:], axis_name, ring_pairs(n, n - 1))
        far = jnp.concatenate([far_a, far_b], axis=0)
        return [x, from_next, far, from_prev]
    recv = [x] + [lax.ppermute(x, axis_name, ring_pairs(n, k)) for k in range(1, n)]
    return [recv[(-m) % n] for m in range(n)]


def ring_gather(x, axis_name):
    return in_order(ring_parts(x, axis_name), axis_name)


def ring_reduce(blocks, axis_name):
    n = lax.axis_size(axis_name)
    me = lax.axis_index(axis_name)

    def blk(k):
        return lax.dynamic_index_in_dim(blocks, (me + k) % n, axis=0, keepdims=False).astype(jnp.float32)

    def send(v, k):
        return lax.ppermute(v.astype(jnp.bfloat16), axis_name, ring_pairs(n, k)).astype(jnp.float32)

    if n == 4:
        far = blk(2)
        half = far.shape[0] // 2
        got_a = send(far[:half], 1)
        got_b = send(far[half:], n - 1)
        nxt = blk(1)
        prv = blk(n - 1)
        nxt = jnp.concatenate([nxt[:half] + got_a, nxt[half:]], axis=0)
        prv = jnp.concatenate([prv[:half], prv[half:] + got_b], axis=0)
        return blk(0) + send(nxt, 1) + send(prv, n - 1)
    total = blk(0)
    for k in range(1, n):
        total = total + send(blk(k), k)
    return total


def local(hidden, combine_weight, down_weight, cotangent, expert_rows, block_expert, slot_token):
    slot_count, hidden_width = hidden.shape
    block_count = block_expert.shape[0]
    n_dp = lax.axis_size(("z", "xl"))
    part_width = cotangent.shape[1]
    positions = jnp.arange(slot_count, dtype=jnp.int32)
    blocks = positions // BLK
    live_rows = expert_rows[0]
    first_blocks = (live_rows[0] + BLK - 1) // BLK
    second_blocks = (live_rows[1] + BLK - 1) // BLK
    live = jnp.where(
        blocks < first_blocks,
        positions < live_rows[0],
        (blocks < first_blocks + second_blocks) & (positions - first_blocks * BLK < live_rows[1]),
    )
    slot_scale = combine_weight * live.astype(jnp.float32)
    slot_expert = jnp.repeat(block_expert, BLK)

    fsdp = ("xh", "y", "core")
    w = down_weight.reshape(down_weight.shape[0], EXPERTS * hidden_width)
    panel = lax.all_gather(w, fsdp, axis=0, tiled=True)
    model_width = panel.shape[0]
    panel_e = [panel[:, e * hidden_width : (e + 1) * hidden_width] for e in range(EXPERTS)]
    panel_parts = [p.reshape(n_dp, model_width // n_dp, hidden_width) for p in panel_e]

    prep = []
    for e in range(EXPERTS):
        valid = live & (slot_expert == e)
        target = jnp.where(valid, slot_token, slot_count)
        inv = jnp.zeros((slot_count,), jnp.int32).at[target].set(positions, mode="drop")
        has = jnp.zeros((slot_count,), jnp.bool_).at[target].set(True, mode="drop")
        scale_e = jnp.where(has, slot_scale[inv], 0.0)
        sel = ((inv[:, None] == positions[None, :]) & has[:, None]).astype(jnp.bfloat16)
        hid_e = jnp.dot(sel, hidden, preferred_element_type=jnp.float32).astype(jnp.bfloat16)
        prep.append((scale_e, hid_e))

    pair = ring_gather(cotangent, "xl")
    parts = ring_parts(pair, "z")
    prep, far = lax.optimization_barrier((prep, parts[2]))
    parts[2] = far
    tok_hot = (slot_token[:, None] == positions[None, :]).astype(jnp.bfloat16)

    lo = (block_count - 1) * BLK
    masks = [slot_expert == e for e in range(EXPERTS)]
    windows = [(0, lo), (BLK, slot_count)]

    rel = []
    grads_rel = [[] for _ in range(EXPERTS)]
    for p in parts:
        picked = jnp.einsum("st,xtc->sxc", tok_hot, p, preferred_element_type=jnp.float32)
        part_cot = (slot_scale[:, None, None] * picked).astype(jnp.bfloat16).reshape(slot_count, -1)
        rel.append(part_cot)
        for e in range(EXPERTS):
            a, b = windows[e]
            cot_w = part_cot[a:b]
            cot_e = jnp.where(masks[e][a:b, None], cot_w, jnp.zeros_like(cot_w))
            grads_rel[e].append(
                jnp.einsum("sd,sh->dh", cot_e, hidden[a:b], preferred_element_type=jnp.float32).astype(
                    jnp.bfloat16
                )
            )
    n_z = lax.axis_size("z")
    z = lax.axis_index("z")
    shift = (n_z - z) % n_z
    slot_cot = lax.dynamic_slice_in_dim(jnp.stack(rel * 2, axis=1), shift, n_z, axis=1).reshape(
        slot_count, model_width
    )
    grads_twice = jnp.stack([jnp.stack(g * 2, axis=0) for g in grads_rel], axis=0)
    device_grad = lax.dynamic_slice_in_dim(grads_twice, shift, n_z, axis=1).reshape(
        EXPERTS, model_width, hidden_width
    )
    device_grad, panel = lax.optimization_barrier((device_grad, panel))
    summed = lax.psum_scatter(device_grad, fsdp, scatter_dimension=1, tiled=True).astype(jnp.float32)
    grad_scale = 1.0 / math.sqrt(lax.axis_size(fsdp) * slot_count)
    grad_down = jnp.transpose((summed * grad_scale).astype(jnp.bfloat16), (1, 0, 2))

    combined = None
    for e in range(EXPERTS):
        scale_e, hid_e = prep[e]
        out_e = jnp.einsum("th,jch->jtc", hid_e, panel_parts[e], preferred_element_type=jnp.float32)
        term = scale_e[None, :, None] * out_e
        combined = term if combined is None else combined + term
    token_part = combined.astype(jnp.bfloat16)
    n_xl = lax.axis_size("xl")
    by_z = ring_reduce(token_part.reshape(n_dp // n_xl, n_xl, slot_count, part_width), "z")
    expert_out = ring_reduce(by_z, "xl").astype(jnp.bfloat16)

    both = jnp.dot(slot_cot, panel, preferred_element_type=jnp.float32)
    hidden_grad = jnp.where(
        masks[0][:, None], both[:, :hidden_width], both[:, hidden_width:]
    ).astype(jnp.bfloat16)
    return (expert_out, hidden_grad, grad_down)


def solution(mesh):
    n_core = 2
    n_fsdp = mesh.shape["fsdp"]
    n_dp = mesh.shape["dp"]
    n_x = 2
    shape = (n_x, n_fsdp // (n_x * n_core), n_core, n_dp // n_x, n_x)
    fine = jax.sharding.Mesh(mesh.devices.reshape(shape), ("xh", "y", "core", "z", "xl"))
    rows = ("xh", "y", "core")
    cols = ("z", "xl")
    in_specs = (
        P(rows, cols),
        P(rows),
        P(rows, None, cols),
        P(rows, cols),
        P(rows, None),
        P(rows),
        P(rows),
    )
    out_specs = (P(rows, cols), P(rows, cols), P(rows, None, cols))
    return jax.shard_map(local, mesh=fine, in_specs=in_specs, out_specs=out_specs, check_vma=False)
```

```python
import math

import jax
import jax.numpy as jnp
from jax import lax
from jax.sharding import PartitionSpec as P

EXPERTS = 2
BLK = 128


def ring_pairs(n, k):
    return [(i, (i + k) % n) for i in range(n)]


def in_order(rel, axis_name):
    n = lax.axis_size(axis_name)
    me = lax.axis_index(axis_name)
    arr = jnp.stack(list(rel) * 2, axis=0)
    return lax.dynamic_slice_in_dim(arr, (n - me) % n, n, axis=0)


def ring_parts(x, axis_name):
    n = lax.axis_size(axis_name)
    if n == 4:
        half = x.shape[0] // 2
        from_prev = lax.ppermute(x, axis_name, ring_pairs(n, 1))
        from_next = lax.ppermute(x, axis_name, ring_pairs(n, n - 1))
        far_a = lax.ppermute(from_prev[:half], axis_name, ring_pairs(n, 1))
        far_b = lax.ppermute(from_next[half:], axis_name, ring_pairs(n, n - 1))
        far = jnp.concatenate([far_a, far_b], axis=0)
        return [x, from_next, far, from_prev]
    recv = [x] + [lax.ppermute(x, axis_name, ring_pairs(n, k)) for k in range(1, n)]
    return [recv[(-m) % n] for m in range(n)]


def ring_gather(x, axis_name):
    return in_order(ring_parts(x, axis_name), axis_name)


def ring_reduce(blocks, axis_name):
    n = lax.axis_size(axis_name)
    me = lax.axis_index(axis_name)

    def blk(k):
        return lax.dynamic_index_in_dim(blocks, (me + k) % n, axis=0, keepdims=False).astype(jnp.float32)

    def send(v, k):
        return lax.ppermute(v.astype(jnp.bfloat16), axis_name, ring_pairs(n, k)).astype(jnp.float32)

    if n == 4:
        far = blk(2)
        half = far.shape[0] // 2
        got_a = send(far[:half], 1)
        got_b = send(far[half:], n - 1)
        nxt = blk(1)
        prv = blk(n - 1)
        nxt = jnp.concatenate([nxt[:half] + got_a, nxt[half:]], axis=0)
        prv = jnp.concatenate([prv[:half], prv[half:] + got_b], axis=0)
        return blk(0) + send(nxt, 1) + send(prv, n - 1)
    total = blk(0)
    for k in range(1, n):
        total = total + send(blk(k), k)
    return total


def local(hidden, combine_weight, down_weight, cotangent, expert_rows, block_expert, slot_token):
    slot_count, hidden_width = hidden.shape
    block_count = block_expert.shape[0]
    n_dp = lax.axis_size(("z", "xl"))
    part_width = cotangent.shape[1]
    positions = jnp.arange(slot_count, dtype=jnp.int32)
    blocks = positions // BLK
    live_rows = expert_rows[0]
    first_blocks = (live_rows[0] + BLK - 1) // BLK
    second_blocks = (live_rows[1] + BLK - 1) // BLK
    live = jnp.where(
        blocks < first_blocks,
        positions < live_rows[0],
        (blocks < first_blocks + second_blocks) & (positions - first_blocks * BLK < live_rows[1]),
    )
    slot_scale = combine_weight * live.astype(jnp.float32)
    slot_expert = jnp.repeat(block_expert, BLK)

    fsdp = ("xh", "y", "core")
    w = down_weight.reshape(down_weight.shape[0], EXPERTS * hidden_width)
    panel = lax.all_gather(w, fsdp, axis=0, tiled=True)
    model_width = panel.shape[0]
    panel_e = [panel[:, e * hidden_width : (e + 1) * hidden_width] for e in range(EXPERTS)]
    panel_parts = [p.reshape(n_dp, model_width // n_dp, hidden_width) for p in panel_e]

    prep = []
    for e in range(EXPERTS):
        valid = live & (slot_expert == e)
        target = jnp.where(valid, slot_token, slot_count)
        inv = jnp.zeros((slot_count,), jnp.int32).at[target].set(positions, mode="drop")
        has = jnp.zeros((slot_count,), jnp.bool_).at[target].set(True, mode="drop")
        scale_e = jnp.where(has, slot_scale[inv], 0.0)
        sel = ((inv[:, None] == positions[None, :]) & has[:, None]).astype(jnp.bfloat16)
        hid_e = jnp.dot(sel, hidden, preferred_element_type=jnp.float32).astype(jnp.bfloat16)
        prep.append((scale_e, hid_e))

    pair = ring_gather(cotangent, "xl")
    parts = ring_parts(pair, "z")
    prep, far = lax.optimization_barrier((prep, parts[2]))
    parts[2] = far
    tok_hot = (slot_token[:, None] == positions[None, :]).astype(jnp.bfloat16)

    lo = (block_count - 1) * BLK
    masks = [slot_expert == e for e in range(EXPERTS)]
    windows = [(0, lo), (BLK, slot_count)]

    rel = []
    grads_rel = [[] for _ in range(EXPERTS)]
    for p in parts:
        picked = jnp.einsum("st,xtc->sxc", tok_hot, p, preferred_element_type=jnp.float32)
        part_cot = (slot_scale[:, None, None] * picked).astype(jnp.bfloat16).reshape(slot_count, -1)
        rel.append(part_cot)
        for e in range(EXPERTS):
            a, b = windows[e]
            cot_w = part_cot[a:b]
            cot_e = jnp.where(masks[e][a:b, None], cot_w, jnp.zeros_like(cot_w))
            grads_rel[e].append(
                jnp.einsum("sd,sh->dh", cot_e, hidden[a:b], preferred_element_type=jnp.float32).astype(
                    jnp.bfloat16
                )
            )
    n_z = lax.axis_size("z")
    z = lax.axis_index("z")
    shift = (n_z - z) % n_z
    slot_cot = lax.dynamic_slice_in_dim(jnp.stack(rel * 2, axis=1), shift, n_z, axis=1).reshape(
        slot_count, model_width
    )
    grads_twice = jnp.stack([jnp.stack(g * 2, axis=0) for g in grads_rel], axis=0)
    device_grad = lax.dynamic_slice_in_dim(grads_twice, shift, n_z, axis=1).reshape(
        EXPERTS, model_width, hidden_width
    )
    n_xh, n_y, n_core = lax.axis_size("xh"), lax.axis_size("y"), lax.axis_size("core")
    xh, core = lax.axis_index("xh"), lax.axis_index("core")
    rows = model_width // (n_xh * n_y * n_core)
    split = device_grad.reshape(EXPERTS, n_xh, n_y, n_core, rows, hidden_width)
    keep = lax.dynamic_index_in_dim(split, core, axis=3, keepdims=False).astype(jnp.float32)
    send = lax.dynamic_index_in_dim(split, (core + 1) % n_core, axis=3, keepdims=False)
    by_core = keep + lax.ppermute(send, "core", ring_pairs(n_core, 1)).astype(jnp.float32)
    y_major = jnp.transpose(by_core.astype(jnp.bfloat16), (2, 0, 1, 3, 4))
    by_y = ring_reduce(y_major, "y")
    keep = lax.dynamic_index_in_dim(by_y, xh, axis=1, keepdims=False).astype(jnp.float32)
    send = lax.dynamic_index_in_dim(by_y, (xh + 1) % n_xh, axis=1, keepdims=False).astype(jnp.bfloat16)
    summed = keep + lax.ppermute(send, "xh", ring_pairs(n_xh, 1)).astype(jnp.float32)
    grad_scale = 1.0 / math.sqrt(lax.axis_size(fsdp) * slot_count)
    grad_down = jnp.transpose((summed * grad_scale).astype(jnp.bfloat16), (1, 0, 2))

    combined = None
    for e in range(EXPERTS):
        scale_e, hid_e = prep[e]
        out_e = jnp.einsum("th,jch->jtc", hid_e, panel_parts[e], preferred_element_type=jnp.float32)
        term = scale_e[None, :, None] * out_e
        combined = term if combined is None else combined + term
    token_part = combined.astype(jnp.bfloat16)
    n_xl = lax.axis_size("xl")
    by_z = ring_reduce(token_part.reshape(n_dp // n_xl, n_xl, slot_count, part_width), "z")
    expert_out = ring_reduce(by_z, "xl").astype(jnp.bfloat16)

    both = jnp.dot(slot_cot, panel, preferred_element_type=jnp.float32)
    hidden_grad = jnp.where(
        masks[0][:, None], both[:, :hidden_width], both[:, hidden_width:]
    ).astype(jnp.bfloat16)
    return (expert_out, hidden_grad, grad_down)


def solution(mesh):
    n_core = 2
    n_fsdp = mesh.shape["fsdp"]
    n_dp = mesh.shape["dp"]
    n_x = 2
    shape = (n_x, n_fsdp // (n_x * n_core), n_core, n_dp // n_x, n_x)
    fine = jax.sharding.Mesh(mesh.devices.reshape(shape), ("xh", "y", "core", "z", "xl"))
    rows = ("xh", "y", "core")
    cols = ("z", "xl")
    in_specs = (
        P(rows, cols),
        P(rows),
        P(rows, None, cols),
        P(rows, cols),
        P(rows, None),
        P(rows),
        P(rows),
    )
    out_specs = (P(rows, cols), P(rows, cols), P(rows, None, cols))
    return jax.shard_map(local, mesh=fine, in_specs=in_specs, out_specs=out_specs, check_vma=False)
```

```python
import math

import jax
import jax.numpy as jnp
from jax import lax
from jax.sharding import PartitionSpec as P

EXPERTS = 2
BLK = 128


def ring_pairs(n, k):
    return [(i, (i + k) % n) for i in range(n)]


def in_order(rel, axis_name):
    n = lax.axis_size(axis_name)
    me = lax.axis_index(axis_name)
    arr = jnp.stack(list(rel) * 2, axis=0)
    return lax.dynamic_slice_in_dim(arr, (n - me) % n, n, axis=0)


def ring_parts(x, axis_name):
    n = lax.axis_size(axis_name)
    if n == 4:
        half = x.shape[0] // 2
        from_prev = lax.ppermute(x, axis_name, ring_pairs(n, 1))
        from_next = lax.ppermute(x, axis_name, ring_pairs(n, n - 1))
        far_a = lax.ppermute(from_prev[:half], axis_name, ring_pairs(n, 1))
        far_b = lax.ppermute(from_next[half:], axis_name, ring_pairs(n, n - 1))
        far = jnp.concatenate([far_a, far_b], axis=0)
        return [x, from_next, far, from_prev]
    recv = [x] + [lax.ppermute(x, axis_name, ring_pairs(n, k)) for k in range(1, n)]
    return [recv[(-m) % n] for m in range(n)]


def ring_gather(x, axis_name):
    return in_order(ring_parts(x, axis_name), axis_name)


def ring_reduce(blocks, axis_name):
    n = lax.axis_size(axis_name)
    me = lax.axis_index(axis_name)

    def blk(k):
        return lax.dynamic_index_in_dim(blocks, (me + k) % n, axis=0, keepdims=False).astype(jnp.float32)

    def send(v, k):
        return lax.ppermute(v.astype(jnp.bfloat16), axis_name, ring_pairs(n, k)).astype(jnp.float32)

    if n == 4:
        far = blk(2)
        half = far.shape[0] // 2
        got_a = send(far[:half], 1)
        got_b = send(far[half:], n - 1)
        nxt = blk(1)
        prv = blk(n - 1)
        nxt = jnp.concatenate([nxt[:half] + got_a, nxt[half:]], axis=0)
        prv = jnp.concatenate([prv[:half], prv[half:] + got_b], axis=0)
        return blk(0) + send(nxt, 1) + send(prv, n - 1)
    total = blk(0)
    for k in range(1, n):
        total = total + send(blk(k), k)
    return total


def local(hidden, combine_weight, down_weight, cotangent, expert_rows, block_expert, slot_token):
    slot_count, hidden_width = hidden.shape
    block_count = block_expert.shape[0]
    n_dp = lax.axis_size(("z", "xl"))
    part_width = cotangent.shape[1]
    positions = jnp.arange(slot_count, dtype=jnp.int32)
    blocks = positions // BLK
    live_rows = expert_rows[0]
    first_blocks = (live_rows[0] + BLK - 1) // BLK
    second_blocks = (live_rows[1] + BLK - 1) // BLK
    live = jnp.where(
        blocks < first_blocks,
        positions < live_rows[0],
        (blocks < first_blocks + second_blocks) & (positions - first_blocks * BLK < live_rows[1]),
    )
    slot_scale = combine_weight * live.astype(jnp.float32)
    slot_expert = jnp.repeat(block_expert, BLK)

    fsdp = ("xh", "y", "core")
    w = down_weight.reshape(down_weight.shape[0], EXPERTS * hidden_width)
    panel = lax.all_gather(w, fsdp, axis=0, tiled=True)
    model_width = panel.shape[0]
    panel_e = [panel[:, e * hidden_width : (e + 1) * hidden_width] for e in range(EXPERTS)]
    panel_parts = [p.reshape(n_dp, model_width // n_dp, hidden_width) for p in panel_e]

    prep = []
    for e in range(EXPERTS):
        valid = live & (slot_expert == e)
        target = jnp.where(valid, slot_token, slot_count)
        inv = jnp.zeros((slot_count,), jnp.int32).at[target].set(positions, mode="drop")
        has = jnp.zeros((slot_count,), jnp.bool_).at[target].set(True, mode="drop")
        scale_e = jnp.where(has, slot_scale[inv], 0.0)
        sel = ((inv[:, None] == positions[None, :]) & has[:, None]).astype(jnp.bfloat16)
        hid_e = jnp.dot(sel, hidden, preferred_element_type=jnp.float32).astype(jnp.bfloat16)
        prep.append((scale_e, hid_e))

    pair = ring_gather(cotangent, "xl")
    parts = ring_parts(pair, "z")
    prep, far = lax.optimization_barrier((prep, parts[2]))
    parts[2] = far
    tok_hot = (slot_token[:, None] == positions[None, :]).astype(jnp.bfloat16)

    lo = (block_count - 1) * BLK
    masks = [slot_expert == e for e in range(EXPERTS)]
    windows = [(0, lo), (BLK, slot_count)]

    rel = []
    grads_rel = [[] for _ in range(EXPERTS)]
    for p in parts:
        picked = jnp.einsum("st,xtc->sxc", tok_hot, p, preferred_element_type=jnp.float32)
        part_cot = (slot_scale[:, None, None] * picked).astype(jnp.bfloat16).reshape(slot_count, -1)
        rel.append(part_cot)
        for e in range(EXPERTS):
            a, b = windows[e]
            cot_w = part_cot[a:b]
            cot_e = jnp.where(masks[e][a:b, None], cot_w, jnp.zeros_like(cot_w))
            grads_rel[e].append(
                jnp.einsum("sd,sh->dh", cot_e, hidden[a:b], preferred_element_type=jnp.float32).astype(
                    jnp.bfloat16
                )
            )
    n_z = lax.axis_size("z")
    z = lax.axis_index("z")
    shift = (n_z - z) % n_z
    slot_cot = lax.dynamic_slice_in_dim(jnp.stack(rel * 2, axis=1), shift, n_z, axis=1).reshape(
        slot_count, model_width
    )
    grads_twice = jnp.stack([jnp.stack(g * 2, axis=0) for g in grads_rel], axis=0)
    device_grad = lax.dynamic_slice_in_dim(grads_twice, shift, n_z, axis=1).reshape(
        EXPERTS, model_width, hidden_width
    )
    n_xh, n_y, n_core = lax.axis_size("xh"), lax.axis_size("y"), lax.axis_size("core")
    xh, core = lax.axis_index("xh"), lax.axis_index("core")
    rows = model_width // (n_xh * n_y * n_core)
    split = device_grad.reshape(EXPERTS, n_xh, n_y, n_core, rows, hidden_width)
    keep = lax.dynamic_index_in_dim(split, core, axis=3, keepdims=False).astype(jnp.float32)
    send = lax.dynamic_index_in_dim(split, (core + 1) % n_core, axis=3, keepdims=False)
    by_core = keep + lax.ppermute(send, "core", ring_pairs(n_core, 1)).astype(jnp.float32)
    combined = None
    for e in range(EXPERTS):
        scale_e, hid_e = prep[e]
        out_e = jnp.einsum("th,jch->jtc", hid_e, panel_parts[e], preferred_element_type=jnp.float32)
        term = scale_e[None, :, None] * out_e
        combined = term if combined is None else combined + term
    token_part = combined.astype(jnp.bfloat16)
    token_part, by_core = lax.optimization_barrier((token_part, by_core))
    y_major = jnp.transpose(by_core.astype(jnp.bfloat16), (2, 0, 1, 3, 4))
    by_y = ring_reduce(y_major, "y")
    keep = lax.dynamic_index_in_dim(by_y, xh, axis=1, keepdims=False).astype(jnp.float32)
    send = lax.dynamic_index_in_dim(by_y, (xh + 1) % n_xh, axis=1, keepdims=False).astype(jnp.bfloat16)
    summed = keep + lax.ppermute(send, "xh", ring_pairs(n_xh, 1)).astype(jnp.float32)
    grad_scale = 1.0 / math.sqrt(lax.axis_size(fsdp) * slot_count)
    grad_down = jnp.transpose((summed * grad_scale).astype(jnp.bfloat16), (1, 0, 2))

    n_xl = lax.axis_size("xl")
    by_z = ring_reduce(token_part.reshape(n_dp // n_xl, n_xl, slot_count, part_width), "z")
    expert_out = ring_reduce(by_z, "xl").astype(jnp.bfloat16)

    both = jnp.dot(slot_cot, panel, preferred_element_type=jnp.float32)
    hidden_grad = jnp.where(
        masks[0][:, None], both[:, :hidden_width], both[:, hidden_width:]
    ).astype(jnp.bfloat16)
    return (expert_out, hidden_grad, grad_down)


def solution(mesh):
    n_core = 2
    n_fsdp = mesh.shape["fsdp"]
    n_dp = mesh.shape["dp"]
    n_x = 2
    shape = (n_x, n_fsdp // (n_x * n_core), n_core, n_dp // n_x, n_x)
    fine = jax.sharding.Mesh(mesh.devices.reshape(shape), ("xh", "y", "core", "z", "xl"))
    rows = ("xh", "y", "core")
    cols = ("z", "xl")
    in_specs = (
        P(rows, cols),
        P(rows),
        P(rows, None, cols),
        P(rows, cols),
        P(rows, None),
        P(rows),
        P(rows),
    )
    out_specs = (P(rows, cols), P(rows, cols), P(rows, None, cols))
    return jax.shard_map(local, mesh=fine, in_specs=in_specs, out_specs=out_specs, check_vma=False)
```

```python
import math

import jax
import jax.numpy as jnp
from jax import lax
from jax.sharding import PartitionSpec as P

EXPERTS = 2
BLK = 128


def ring_pairs(n, k):
    return [(i, (i + k) % n) for i in range(n)]


def in_order(rel, axis_name):
    n = lax.axis_size(axis_name)
    me = lax.axis_index(axis_name)
    arr = jnp.stack(list(rel) * 2, axis=0)
    return lax.dynamic_slice_in_dim(arr, (n - me) % n, n, axis=0)


def ring_parts(x, axis_name):
    n = lax.axis_size(axis_name)
    if n == 4:
        half = x.shape[0] // 2
        from_prev = lax.ppermute(x, axis_name, ring_pairs(n, 1))
        from_next = lax.ppermute(x, axis_name, ring_pairs(n, n - 1))
        far_a = lax.ppermute(from_prev[:half], axis_name, ring_pairs(n, 1))
        far_b = lax.ppermute(from_next[half:], axis_name, ring_pairs(n, n - 1))
        far = jnp.concatenate([far_a, far_b], axis=0)
        return [x, from_next, far, from_prev]
    recv = [x] + [lax.ppermute(x, axis_name, ring_pairs(n, k)) for k in range(1, n)]
    return [recv[(-m) % n] for m in range(n)]


def ring_gather(x, axis_name):
    return in_order(ring_parts(x, axis_name), axis_name)


def ring_reduce(blocks, axis_name):
    n = lax.axis_size(axis_name)
    me = lax.axis_index(axis_name)

    def blk(k):
        return lax.dynamic_index_in_dim(blocks, (me + k) % n, axis=0, keepdims=False).astype(jnp.float32)

    def send(v, k):
        return lax.ppermute(v.astype(jnp.bfloat16), axis_name, ring_pairs(n, k)).astype(jnp.float32)

    if n == 4:
        far = blk(2)
        half = far.shape[0] // 2
        got_a = send(far[:half], 1)
        got_b = send(far[half:], n - 1)
        nxt = blk(1)
        prv = blk(n - 1)
        nxt = jnp.concatenate([nxt[:half] + got_a, nxt[half:]], axis=0)
        prv = jnp.concatenate([prv[:half], prv[half:] + got_b], axis=0)
        return blk(0) + send(nxt, 1) + send(prv, n - 1)
    total = blk(0)
    for k in range(1, n):
        total = total + send(blk(k), k)
    return total


def local(hidden, combine_weight, down_weight, cotangent, expert_rows, block_expert, slot_token):
    slot_count, hidden_width = hidden.shape
    block_count = block_expert.shape[0]
    n_dp = lax.axis_size(("z", "xl"))
    part_width = cotangent.shape[1]
    positions = jnp.arange(slot_count, dtype=jnp.int32)
    blocks = positions // BLK
    live_rows = expert_rows[0]
    first_blocks = (live_rows[0] + BLK - 1) // BLK
    second_blocks = (live_rows[1] + BLK - 1) // BLK
    live = jnp.where(
        blocks < first_blocks,
        positions < live_rows[0],
        (blocks < first_blocks + second_blocks) & (positions - first_blocks * BLK < live_rows[1]),
    )
    slot_scale = combine_weight * live.astype(jnp.float32)
    slot_expert = jnp.repeat(block_expert, BLK)

    fsdp = ("xh", "y", "core")
    w = down_weight.reshape(down_weight.shape[0], EXPERTS * hidden_width)
    panel = lax.all_gather(w, fsdp, axis=0, tiled=True)
    model_width = panel.shape[0]
    panel_e = [panel[:, e * hidden_width : (e + 1) * hidden_width] for e in range(EXPERTS)]
    panel_parts = [p.reshape(n_dp, model_width // n_dp, hidden_width) for p in panel_e]

    prep = []
    for e in range(EXPERTS):
        valid = live & (slot_expert == e)
        target = jnp.where(valid, slot_token, slot_count)
        inv = jnp.zeros((slot_count,), jnp.int32).at[target].set(positions, mode="drop")
        has = jnp.zeros((slot_count,), jnp.bool_).at[target].set(True, mode="drop")
        scale_e = jnp.where(has, slot_scale[inv], 0.0)
        sel = ((inv[:, None] == positions[None, :]) & has[:, None]).astype(jnp.bfloat16)
        hid_e = jnp.dot(sel, hidden, preferred_element_type=jnp.float32).astype(jnp.bfloat16)
        prep.append((scale_e, hid_e))

    pair = ring_gather(cotangent, "xl")
    parts = ring_parts(pair, "z")
    prep, far = lax.optimization_barrier((prep, parts[2]))
    parts[2] = far
    tok_hot = (slot_token[:, None] == positions[None, :]).astype(jnp.bfloat16)

    lo = (block_count - 1) * BLK
    masks = [slot_expert == e for e in range(EXPERTS)]
    windows = [(0, lo), (BLK, slot_count)]

    rel = []
    grads_rel = [[] for _ in range(EXPERTS)]
    for p in parts:
        picked = jnp.einsum("st,xtc->sxc", tok_hot, p, preferred_element_type=jnp.float32)
        part_cot = (slot_scale[:, None, None] * picked).astype(jnp.bfloat16).reshape(slot_count, -1)
        rel.append(part_cot)
        for e in range(EXPERTS):
            a, b = windows[e]
            cot_w = part_cot[a:b]
            cot_e = jnp.where(masks[e][a:b, None], cot_w, jnp.zeros_like(cot_w))
            grads_rel[e].append(
                jnp.einsum("sd,sh->dh", cot_e, hidden[a:b], preferred_element_type=jnp.float32).astype(
                    jnp.bfloat16
                )
            )
    n_z = lax.axis_size("z")
    z = lax.axis_index("z")
    shift = (n_z - z) % n_z
    slot_cot = lax.dynamic_slice_in_dim(jnp.stack(rel * 2, axis=1), shift, n_z, axis=1).reshape(
        slot_count, model_width
    )
    grads_twice = jnp.stack([jnp.stack(g * 2, axis=0) for g in grads_rel], axis=0)
    device_grad = lax.dynamic_slice_in_dim(grads_twice, shift, n_z, axis=1).reshape(
        EXPERTS, model_width, hidden_width
    )
    device_grad, panel = lax.optimization_barrier((device_grad, panel))
    sc_part = lax.psum_scatter(device_grad[:1], fsdp, scatter_dimension=1, tiled=True).astype(jnp.float32)
    n_xh, n_y, n_core = lax.axis_size("xh"), lax.axis_size("y"), lax.axis_size("core")
    xh, core = lax.axis_index("xh"), lax.axis_index("core")
    rows = model_width // (n_xh * n_y * n_core)
    split = device_grad[1:].reshape(1, n_xh, n_y, n_core, rows, hidden_width)
    keep = lax.dynamic_index_in_dim(split, core, axis=3, keepdims=False).astype(jnp.float32)
    send = lax.dynamic_index_in_dim(split, (core + 1) % n_core, axis=3, keepdims=False)
    by_core = keep + lax.ppermute(send, "core", ring_pairs(n_core, 1)).astype(jnp.float32)
    y_major = jnp.transpose(by_core.astype(jnp.bfloat16), (2, 0, 1, 3, 4))
    by_y = ring_reduce(jnp.swapaxes(y_major, 1, 2), "y")
    keep = lax.dynamic_index_in_dim(by_y, xh, axis=0, keepdims=False).astype(jnp.float32)
    send = lax.dynamic_index_in_dim(by_y, (xh + 1) % n_xh, axis=0, keepdims=False).astype(jnp.bfloat16)
    pp_part = keep + lax.ppermute(send, "xh", ring_pairs(n_xh, 1)).astype(jnp.float32)
    summed = jnp.concatenate([sc_part, pp_part], axis=0)
    grad_scale = 1.0 / math.sqrt(lax.axis_size(fsdp) * slot_count)
    grad_down = jnp.transpose((summed * grad_scale).astype(jnp.bfloat16), (1, 0, 2))

    combined = None
    for e in range(EXPERTS):
        scale_e, hid_e = prep[e]
        out_e = jnp.einsum("th,jch->jtc", hid_e, panel_parts[e], preferred_element_type=jnp.float32)
        term = scale_e[None, :, None] * out_e
        combined = term if combined is None else combined + term
    token_part = combined.astype(jnp.bfloat16)
    n_xl = lax.axis_size("xl")
    by_z = ring_reduce(token_part.reshape(n_dp // n_xl, n_xl, slot_count, part_width), "z")
    expert_out = ring_reduce(by_z, "xl").astype(jnp.bfloat16)

    both = jnp.dot(slot_cot, panel, preferred_element_type=jnp.float32)
    hidden_grad = jnp.where(
        masks[0][:, None], both[:, :hidden_width], both[:, hidden_width:]
    ).astype(jnp.bfloat16)
    return (expert_out, hidden_grad, grad_down)


def solution(mesh):
    n_core = 2
    n_fsdp = mesh.shape["fsdp"]
    n_dp = mesh.shape["dp"]
    n_x = 2
    shape = (n_x, n_fsdp // (n_x * n_core), n_core, n_dp // n_x, n_x)
    fine = jax.sharding.Mesh(mesh.devices.reshape(shape), ("xh", "y", "core", "z", "xl"))
    rows = ("xh", "y", "core")
    cols = ("z", "xl")
    in_specs = (
        P(rows, cols),
        P(rows),
        P(rows, None, cols),
        P(rows, cols),
        P(rows, None),
        P(rows),
        P(rows),
    )
    out_specs = (P(rows, cols), P(rows, cols), P(rows, None, cols))
    return jax.shard_map(local, mesh=fine, in_specs=in_specs, out_specs=out_specs, check_vma=False)
```

```python
import math

import jax
import jax.numpy as jnp
from jax import lax
from jax.sharding import PartitionSpec as P

EXPERTS = 2
BLK = 128


def ring_pairs(n, k):
    return [(i, (i + k) % n) for i in range(n)]


def in_order(rel, axis_name):
    n = lax.axis_size(axis_name)
    me = lax.axis_index(axis_name)
    arr = jnp.stack(list(rel) * 2, axis=0)
    return lax.dynamic_slice_in_dim(arr, (n - me) % n, n, axis=0)


def ring_parts(x, axis_name):
    n = lax.axis_size(axis_name)
    if n == 4:
        half = x.shape[0] // 2
        from_prev = lax.ppermute(x, axis_name, ring_pairs(n, 1))
        from_next = lax.ppermute(x, axis_name, ring_pairs(n, n - 1))
        far_a = lax.ppermute(from_prev[:half], axis_name, ring_pairs(n, 1))
        far_b = lax.ppermute(from_next[half:], axis_name, ring_pairs(n, n - 1))
        far = jnp.concatenate([far_a, far_b], axis=0)
        return [x, from_next, far, from_prev]
    recv = [x] + [lax.ppermute(x, axis_name, ring_pairs(n, k)) for k in range(1, n)]
    return [recv[(-m) % n] for m in range(n)]


def ring_gather(x, axis_name):
    return in_order(ring_parts(x, axis_name), axis_name)


def ring_reduce(blocks, axis_name):
    n = lax.axis_size(axis_name)
    me = lax.axis_index(axis_name)

    def blk(k):
        return lax.dynamic_index_in_dim(blocks, (me + k) % n, axis=0, keepdims=False).astype(jnp.float32)

    def send(v, k):
        return lax.ppermute(v.astype(jnp.bfloat16), axis_name, ring_pairs(n, k)).astype(jnp.float32)

    if n == 4:
        far = blk(2)
        half = far.shape[0] // 2
        got_a = send(far[:half], 1)
        got_b = send(far[half:], n - 1)
        nxt = blk(1)
        prv = blk(n - 1)
        nxt = jnp.concatenate([nxt[:half] + got_a, nxt[half:]], axis=0)
        prv = jnp.concatenate([prv[:half], prv[half:] + got_b], axis=0)
        return blk(0) + send(nxt, 1) + send(prv, n - 1)
    total = blk(0)
    for k in range(1, n):
        total = total + send(blk(k), k)
    return total


def local(hidden, combine_weight, down_weight, cotangent, expert_rows, block_expert, slot_token):
    slot_count, hidden_width = hidden.shape
    block_count = block_expert.shape[0]
    n_dp = lax.axis_size(("z", "xl"))
    part_width = cotangent.shape[1]
    positions = jnp.arange(slot_count, dtype=jnp.int32)
    blocks = positions // BLK
    live_rows = expert_rows[0]
    first_blocks = (live_rows[0] + BLK - 1) // BLK
    second_blocks = (live_rows[1] + BLK - 1) // BLK
    live = jnp.where(
        blocks < first_blocks,
        positions < live_rows[0],
        (blocks < first_blocks + second_blocks) & (positions - first_blocks * BLK < live_rows[1]),
    )
    slot_scale = combine_weight * live.astype(jnp.float32)
    slot_expert = jnp.repeat(block_expert, BLK)

    fsdp = ("xh", "y", "core")
    w = down_weight.reshape(down_weight.shape[0], EXPERTS * hidden_width)
    panel = lax.all_gather(w, fsdp, axis=0, tiled=True)
    model_width = panel.shape[0]
    panel_e = [panel[:, e * hidden_width : (e + 1) * hidden_width] for e in range(EXPERTS)]
    panel_parts = [p.reshape(n_dp, model_width // n_dp, hidden_width) for p in panel_e]

    prep = []
    for e in range(EXPERTS):
        valid = live & (slot_expert == e)
        target = jnp.where(valid, slot_token, slot_count)
        inv = jnp.zeros((slot_count,), jnp.int32).at[target].set(positions, mode="drop")
        has = jnp.zeros((slot_count,), jnp.bool_).at[target].set(True, mode="drop")
        scale_e = jnp.where(has, slot_scale[inv], 0.0)
        sel = ((inv[:, None] == positions[None, :]) & has[:, None]).astype(jnp.bfloat16)
        hid_e = jnp.dot(sel, hidden, preferred_element_type=jnp.float32).astype(jnp.bfloat16)
        prep.append((scale_e, hid_e))

    pair = ring_gather(cotangent, "xl")
    parts = ring_parts(pair, "z")
    prep, far = lax.optimization_barrier((prep, parts[2]))
    parts[2] = far
    tok_hot = (slot_token[:, None] == positions[None, :]).astype(jnp.bfloat16)

    lo = (block_count - 1) * BLK
    masks = [slot_expert == e for e in range(EXPERTS)]
    windows = [(0, lo), (BLK, slot_count)]

    rel = []
    grads_rel = [[] for _ in range(EXPERTS)]
    for p in parts:
        picked = jnp.einsum("st,xtc->sxc", tok_hot, p, preferred_element_type=jnp.float32)
        part_cot = (slot_scale[:, None, None] * picked).astype(jnp.bfloat16).reshape(slot_count, -1)
        rel.append(part_cot)
        for e in range(EXPERTS):
            a, b = windows[e]
            cot_w = part_cot[a:b]
            cot_e = jnp.where(masks[e][a:b, None], cot_w, jnp.zeros_like(cot_w))
            grads_rel[e].append(
                jnp.einsum("sd,sh->dh", cot_e, hidden[a:b], preferred_element_type=jnp.float32).astype(
                    jnp.bfloat16
                )
            )
    n_z = lax.axis_size("z")
    z = lax.axis_index("z")
    shift = (n_z - z) % n_z
    slot_cot = lax.dynamic_slice_in_dim(jnp.stack(rel * 2, axis=1), shift, n_z, axis=1).reshape(
        slot_count, model_width
    )
    grads_twice = jnp.stack([jnp.stack(g * 2, axis=0) for g in grads_rel], axis=0)
    device_grad = lax.dynamic_slice_in_dim(grads_twice, shift, n_z, axis=1).reshape(
        EXPERTS, model_width, hidden_width
    )
    device_grad, panel = lax.optimization_barrier((device_grad, panel))
    cut = hidden_width * 3 // 4
    sc_part = lax.psum_scatter(device_grad[..., :cut], fsdp, scatter_dimension=1, tiled=True).astype(
        jnp.float32
    )
    n_xh, n_y, n_core = lax.axis_size("xh"), lax.axis_size("y"), lax.axis_size("core")
    xh, core = lax.axis_index("xh"), lax.axis_index("core")
    rows = model_width // (n_xh * n_y * n_core)
    split = device_grad[..., cut:].reshape(EXPERTS, n_xh, n_y, n_core, rows, hidden_width - cut)
    keep = lax.dynamic_index_in_dim(split, core, axis=3, keepdims=False).astype(jnp.float32)
    send = lax.dynamic_index_in_dim(split, (core + 1) % n_core, axis=3, keepdims=False)
    by_core = keep + lax.ppermute(send, "core", ring_pairs(n_core, 1)).astype(jnp.float32)
    y_major = jnp.transpose(by_core.astype(jnp.bfloat16), (2, 0, 1, 3, 4))
    by_y = ring_reduce(jnp.swapaxes(y_major, 1, 2), "y")
    keep = lax.dynamic_index_in_dim(by_y, xh, axis=0, keepdims=False).astype(jnp.float32)
    send = lax.dynamic_index_in_dim(by_y, (xh + 1) % n_xh, axis=0, keepdims=False).astype(jnp.bfloat16)
    pp_part = keep + lax.ppermute(send, "xh", ring_pairs(n_xh, 1)).astype(jnp.float32)
    summed = jnp.concatenate([sc_part, pp_part], axis=2)
    grad_scale = 1.0 / math.sqrt(lax.axis_size(fsdp) * slot_count)
    grad_down = jnp.transpose((summed * grad_scale).astype(jnp.bfloat16), (1, 0, 2))

    combined = None
    for e in range(EXPERTS):
        scale_e, hid_e = prep[e]
        out_e = jnp.einsum("th,jch->jtc", hid_e, panel_parts[e], preferred_element_type=jnp.float32)
        term = scale_e[None, :, None] * out_e
        combined = term if combined is None else combined + term
    token_part = combined.astype(jnp.bfloat16)
    n_xl = lax.axis_size("xl")
    by_z = ring_reduce(token_part.reshape(n_dp // n_xl, n_xl, slot_count, part_width), "z")
    expert_out = ring_reduce(by_z, "xl").astype(jnp.bfloat16)

    both = jnp.dot(slot_cot, panel, preferred_element_type=jnp.float32)
    hidden_grad = jnp.where(
        masks[0][:, None], both[:, :hidden_width], both[:, hidden_width:]
    ).astype(jnp.bfloat16)
    return (expert_out, hidden_grad, grad_down)


def solution(mesh):
    n_core = 2
    n_fsdp = mesh.shape["fsdp"]
    n_dp = mesh.shape["dp"]
    n_x = 2
    shape = (n_x, n_fsdp // (n_x * n_core), n_core, n_dp // n_x, n_x)
    fine = jax.sharding.Mesh(mesh.devices.reshape(shape), ("xh", "y", "core", "z", "xl"))
    rows = ("xh", "y", "core")
    cols = ("z", "xl")
    in_specs = (
        P(rows, cols),
        P(rows),
        P(rows, None, cols),
        P(rows, cols),
        P(rows, None),
        P(rows),
        P(rows),
    )
    out_specs = (P(rows, cols), P(rows, cols), P(rows, None, cols))
    return jax.shard_map(local, mesh=fine, in_specs=in_specs, out_specs=out_specs, check_vma=False)
```

```python
import math

import jax
import jax.numpy as jnp
from jax import lax
from jax.sharding import PartitionSpec as P

EXPERTS = 2
BLK = 128


def ring_pairs(n, k):
    return [(i, (i + k) % n) for i in range(n)]


def in_order(rel, axis_name):
    n = lax.axis_size(axis_name)
    me = lax.axis_index(axis_name)
    arr = jnp.stack(list(rel) * 2, axis=0)
    return lax.dynamic_slice_in_dim(arr, (n - me) % n, n, axis=0)


def ring_parts(x, axis_name):
    n = lax.axis_size(axis_name)
    if n == 4:
        half = x.shape[0] // 2
        from_prev = lax.ppermute(x, axis_name, ring_pairs(n, 1))
        from_next = lax.ppermute(x, axis_name, ring_pairs(n, n - 1))
        far_a = lax.ppermute(from_prev[:half], axis_name, ring_pairs(n, 1))
        far_b = lax.ppermute(from_next[half:], axis_name, ring_pairs(n, n - 1))
        far = jnp.concatenate([far_a, far_b], axis=0)
        return [x, from_next, far, from_prev]
    recv = [x] + [lax.ppermute(x, axis_name, ring_pairs(n, k)) for k in range(1, n)]
    return [recv[(-m) % n] for m in range(n)]


def ring_gather(x, axis_name):
    return in_order(ring_parts(x, axis_name), axis_name)


def ring_reduce(blocks, axis_name):
    n = lax.axis_size(axis_name)
    me = lax.axis_index(axis_name)

    def blk(k):
        return lax.dynamic_index_in_dim(blocks, (me + k) % n, axis=0, keepdims=False).astype(jnp.float32)

    def send(v, k):
        return lax.ppermute(v.astype(jnp.bfloat16), axis_name, ring_pairs(n, k)).astype(jnp.float32)

    if n == 4:
        far = blk(2)
        half = far.shape[0] // 2
        got_a = send(far[:half], 1)
        got_b = send(far[half:], n - 1)
        nxt = blk(1)
        prv = blk(n - 1)
        nxt = jnp.concatenate([nxt[:half] + got_a, nxt[half:]], axis=0)
        prv = jnp.concatenate([prv[:half], prv[half:] + got_b], axis=0)
        return blk(0) + send(nxt, 1) + send(prv, n - 1)
    total = blk(0)
    for k in range(1, n):
        total = total + send(blk(k), k)
    return total


def local(hidden, combine_weight, down_weight, cotangent, expert_rows, block_expert, slot_token):
    slot_count, hidden_width = hidden.shape
    block_count = block_expert.shape[0]
    n_dp = lax.axis_size(("z", "xl"))
    part_width = cotangent.shape[1]
    positions = jnp.arange(slot_count, dtype=jnp.int32)
    blocks = positions // BLK
    live_rows = expert_rows[0]
    first_blocks = (live_rows[0] + BLK - 1) // BLK
    second_blocks = (live_rows[1] + BLK - 1) // BLK
    live = jnp.where(
        blocks < first_blocks,
        positions < live_rows[0],
        (blocks < first_blocks + second_blocks) & (positions - first_blocks * BLK < live_rows[1]),
    )
    slot_scale = combine_weight * live.astype(jnp.float32)
    slot_expert = jnp.repeat(block_expert, BLK)

    fsdp = ("xh", "y", "core")
    w = down_weight.reshape(down_weight.shape[0], EXPERTS * hidden_width)
    panel = lax.all_gather(w, fsdp, axis=0, tiled=True)
    model_width = panel.shape[0]
    panel_e = [panel[:, e * hidden_width : (e + 1) * hidden_width] for e in range(EXPERTS)]
    panel_parts = [p.reshape(n_dp, model_width // n_dp, hidden_width) for p in panel_e]

    prep = []
    for e in range(EXPERTS):
        valid = live & (slot_expert == e)
        target = jnp.where(valid, slot_token, slot_count)
        inv = jnp.zeros((slot_count,), jnp.int32).at[target].set(positions, mode="drop")
        has = jnp.zeros((slot_count,), jnp.bool_).at[target].set(True, mode="drop")
        scale_e = jnp.where(has, slot_scale[inv], 0.0)
        sel = ((inv[:, None] == positions[None, :]) & has[:, None]).astype(jnp.bfloat16)
        hid_e = jnp.dot(sel, hidden, preferred_element_type=jnp.float32).astype(jnp.bfloat16)
        prep.append((scale_e, hid_e))

    pair = ring_gather(cotangent, "xl")
    parts = ring_parts(pair, "z")
    prep, far = lax.optimization_barrier((prep, parts[2]))
    parts[2] = far
    tok_hot = (slot_token[:, None] == positions[None, :]).astype(jnp.bfloat16)

    lo = (block_count - 1) * BLK
    masks = [slot_expert == e for e in range(EXPERTS)]
    windows = [(0, lo), (BLK, slot_count)]

    cut = hidden_width * 3 // 4
    spans = [(0, cut), (cut, hidden_width)]
    rel = []
    grads_rel = [[[] for _ in range(EXPERTS)] for _ in spans]
    for p in parts:
        picked = jnp.einsum("st,xtc->sxc", tok_hot, p, preferred_element_type=jnp.float32)
        part_cot = (slot_scale[:, None, None] * picked).astype(jnp.bfloat16).reshape(slot_count, -1)
        rel.append(part_cot)
        for e in range(EXPERTS):
            a, b = windows[e]
            cot_w = part_cot[a:b]
            cot_e = jnp.where(masks[e][a:b, None], cot_w, jnp.zeros_like(cot_w))
            for k, (u, v) in enumerate(spans):
                grads_rel[k][e].append(
                    jnp.einsum(
                        "sd,sh->dh", cot_e, hidden[a:b, u:v], preferred_element_type=jnp.float32
                    ).astype(jnp.bfloat16)
                )
    n_z = lax.axis_size("z")
    z = lax.axis_index("z")
    shift = (n_z - z) % n_z
    slot_cot = lax.dynamic_slice_in_dim(jnp.stack(rel * 2, axis=1), shift, n_z, axis=1).reshape(
        slot_count, model_width
    )
    split_grads = []
    for k, (u, v) in enumerate(spans):
        twice = jnp.stack([jnp.stack(g * 2, axis=0) for g in grads_rel[k]], axis=0)
        split_grads.append(
            lax.dynamic_slice_in_dim(twice, shift, n_z, axis=1).reshape(EXPERTS, model_width, v - u)
        )
    sc_grad, pp_grad = split_grads
    sc_grad, panel = lax.optimization_barrier((sc_grad, panel))
    sc_part = lax.psum_scatter(sc_grad, fsdp, scatter_dimension=1, tiled=True).astype(jnp.float32)
    n_xh, n_y, n_core = lax.axis_size("xh"), lax.axis_size("y"), lax.axis_size("core")
    xh, core = lax.axis_index("xh"), lax.axis_index("core")
    rows = model_width // (n_xh * n_y * n_core)
    split = pp_grad.reshape(EXPERTS, n_xh, n_y, n_core, rows, hidden_width - cut)
    keep = lax.dynamic_index_in_dim(split, core, axis=3, keepdims=False).astype(jnp.float32)
    send = lax.dynamic_index_in_dim(split, (core + 1) % n_core, axis=3, keepdims=False)
    by_core = keep + lax.ppermute(send, "core", ring_pairs(n_core, 1)).astype(jnp.float32)
    y_major = jnp.transpose(by_core.astype(jnp.bfloat16), (2, 0, 1, 3, 4))
    by_y = ring_reduce(jnp.swapaxes(y_major, 1, 2), "y")
    keep = lax.dynamic_index_in_dim(by_y, xh, axis=0, keepdims=False).astype(jnp.float32)
    send = lax.dynamic_index_in_dim(by_y, (xh + 1) % n_xh, axis=0, keepdims=False).astype(jnp.bfloat16)
    pp_part = keep + lax.ppermute(send, "xh", ring_pairs(n_xh, 1)).astype(jnp.float32)
    summed = jnp.concatenate([sc_part, pp_part], axis=2)
    grad_scale = 1.0 / math.sqrt(lax.axis_size(fsdp) * slot_count)
    grad_down = jnp.transpose((summed * grad_scale).astype(jnp.bfloat16), (1, 0, 2))

    combined = None
    for e in range(EXPERTS):
        scale_e, hid_e = prep[e]
        out_e = jnp.einsum("th,jch->jtc", hid_e, panel_parts[e], preferred_element_type=jnp.float32)
        term = scale_e[None, :, None] * out_e
        combined = term if combined is None else combined + term
    token_part = combined.astype(jnp.bfloat16)
    n_xl = lax.axis_size("xl")
    by_z = ring_reduce(token_part.reshape(n_dp // n_xl, n_xl, slot_count, part_width), "z")
    expert_out = ring_reduce(by_z, "xl").astype(jnp.bfloat16)

    both = jnp.dot(slot_cot, panel, preferred_element_type=jnp.float32)
    hidden_grad = jnp.where(
        masks[0][:, None], both[:, :hidden_width], both[:, hidden_width:]
    ).astype(jnp.bfloat16)
    return (expert_out, hidden_grad, grad_down)


def solution(mesh):
    n_core = 2
    n_fsdp = mesh.shape["fsdp"]
    n_dp = mesh.shape["dp"]
    n_x = 2
    shape = (n_x, n_fsdp // (n_x * n_core), n_core, n_dp // n_x, n_x)
    fine = jax.sharding.Mesh(mesh.devices.reshape(shape), ("xh", "y", "core", "z", "xl"))
    rows = ("xh", "y", "core")
    cols = ("z", "xl")
    in_specs = (
        P(rows, cols),
        P(rows),
        P(rows, None, cols),
        P(rows, cols),
        P(rows, None),
        P(rows),
        P(rows),
    )
    out_specs = (P(rows, cols), P(rows, cols), P(rows, None, cols))
    return jax.shard_map(local, mesh=fine, in_specs=in_specs, out_specs=out_specs, check_vma=False)
```
